32 devices in a mesh: ctx: 4 (over y, core), uly: 4 (over z), dp: 2 (over x).
Axes of the slice: x: 2, y: 2, z: 4, core: 2. Of those that a mesh axis runs over, the one named last changes fastest.
Arguments:
- queries: bfloat16 [4096, 4096], P(('dp', 'ctx', 'uly')), parts along dimension 0, may hold values from -110 to 110
- key_vectors: bfloat16 [4096, 512], P(('dp', 'ctx', 'uly')), parts along dimension 0, may hold values from -4 to 4
- value_vectors: bfloat16 [4096, 512], P(('dp', 'ctx', 'uly')), parts along dimension 0, may hold values from -6 to 6
- output_grad: bfloat16 [4096, 4096], P(('dp', 'ctx', 'uly')), parts along dimension 0, may hold values from -2 to 2
- doc_lengths: int32 [32], P('dp'), parts along dimension 0, may hold values from 1 to 256, 2048 in all
Outputs:
- query_grad: bfloat16 [4096, 4096], P(('dp', 'ctx', 'uly')), parts along dimension 0
- key_grad: bfloat16 [4096, 512], P(('dp', 'ctx', 'uly')), parts along dimension 0
The draws below stay inside these ranges and needn't reach their ends.
There are 2 independent parts, one for each index of `dp`. The reference program is written for one: setup_inputs(seed, part) draws one part's arguments, and reference() takes and returns one part's arrays. A program takes and returns all parts, laid end to end along the dimension named above; each array names one. Nothing has to cross between parts.
Inputs may be any that keep to these rules, and one draw needn't show every extreme that they name: `doc_lengths`: the 16 lengths sum to 2048, and the longest is exactly 256.
All inputs are finite; a program needn't handle non-finite values.
Results may differ from the reference program's by a relative error of at most 0.015.
Values may be sent and summed in bfloat16 or wider, within the bound.
No kernel may reach another device: no remote copies, remote signals or barrier semaphores. Data moves between devices by JAX's collectives and lax.ppermute only.
A program may use at most 64 MiB of HBM per device.

```python
import math
import jax
import jax.numpy as jnp
import numpy as np
from jax import lax

QH = 32
KVH = 4
HD = 128
GROUP = 8
TOK_DEV = 128
SEQ = 2048
NDOCS = 16
MAXDOC = 256


def draw_pair(key):
    folded = jax.random.fold_in(key, 7)
    query_key, vector_key = jax.random.split(folded)
    queries = jax.random.truncated_normal(query_key, -4.0, 4.0, (SEQ, QH * HD), jnp.float32)
    keys_f = jax.random.truncated_normal(vector_key, -4.0, 4.0, (SEQ, KVH * HD), jnp.float32)
    return (queries, keys_f)


def draw_queries(key, part):
    return draw_pair(key)[0].astype(jnp.bfloat16)


def draw_key_vectors(key, part):
    return draw_pair(key)[1].astype(jnp.bfloat16)


def block_levels(own_key, extent, cuts, low, largest):
    loudness, own = 1.0, jax.random.fold_in(own_key, 6)
    for axis_at, parts in cuts:
        draws = jnp.exp(jax.random.uniform(jax.random.fold_in(own, axis_at), (parts,), jnp.float32, low / len(cuts), largest / len(cuts)))
        loudness = loudness * jnp.repeat(draws, extent[axis_at] // parts).reshape([-1 if axis == axis_at else 1 for axis in range(len(extent))])
    return loudness


def length_profile(number_of, total, reach, slope):
    weights = [(1 << 20) // math.isqrt(rank ** slope) + 1 for rank in range(2, number_of + 1)]
    surplus, counts = total - reach - (number_of - 1), [1] * (number_of - 1)
    while surplus > 0:
        candidates = [i for i in range(number_of - 1) if counts[i] < reach]
        whole, left = sum([weights[i] for i in candidates]), surplus
        for i in candidates:
            addition = min(reach - counts[i], max(1, left * weights[i] // whole), surplus)
            counts[i] = counts[i] + addition
            surplus = surplus - addition
    return np.array([reach] + counts)


def uneven_parts(own_key, count, total, most, slope):
    if count == 2:
        one = jax.random.randint(own_key, (), max(1, total - most), min(most, total - 1) + 1)
        return jnp.stack([one, total - one])
    tallies = jnp.asarray(length_profile(count, total, most, slope), jnp.int32)
    couples = (count - 1) // 2
    giver, taker = tallies[1:1 + 2 * couples:2], tallies[2:2 + 2 * couples:2]
    room = jnp.minimum(giver - 1, most - taker)
    shifted = jax.random.randint(jax.random.fold_in(own_key, 1), (couples,), 0, 1 << 20) % (room + 1)
    tallies = tallies.at[1:1 + 2 * couples:2].set(giver - shifted).at[2:2 + 2 * couples:2].set(taker + shifted)
    return tallies[jax.random.permutation(jax.random.fold_in(own_key, 2), count)]


def scatter_about(key, dims, width, most, cuts=(), held_as=jnp.bfloat16):
    level = block_levels(key, dims, cuts, -0.22, 0.18) if cuts else 1.0
    values = jax.random.normal(key, dims, jnp.float32) * width * level
    return jnp.minimum(jnp.maximum(values, -most), most).astype(held_as)


def setup_inputs(seed: int = 0, part: int = 0) -> dict:
    arg_keys = jax.random.split(jax.random.key(seed), 6)
    own_keys = jax.random.split(jax.random.fold_in(arg_keys[5], part), 6)
    queries = draw_queries(jax.random.fold_in(jax.random.fold_in(arg_keys[5], part), 71), part)
    key_vectors = draw_key_vectors(jax.random.fold_in(jax.random.fold_in(arg_keys[5], part), 71), part)
    value_vectors = scatter_about(own_keys[2], (SEQ, KVH * HD), 1.0, 6.0, ((0, 16),))
    output_grad = scatter_about(own_keys[3], (SEQ, QH * HD), 0.3, 2.0, ((0, 16),))
    doc_lengths = uneven_parts(own_keys[4], NDOCS, SEQ, MAXDOC, 2).astype(jnp.int32)
    return {"queries": queries, "key_vectors": key_vectors, "value_vectors": value_vectors, "output_grad": output_grad, "doc_lengths": doc_lengths}


def doc_index(doc_lengths, positions):
    doc_ends = jnp.cumsum(doc_lengths)
    counted = jnp.sum((positions[:, None] >= doc_ends[None, :]).astype(jnp.int32), axis=1)
    return jnp.where(positions < 0, -1, counted).astype(jnp.int32)


def window_grads(query_block, grad_block, key_window, value_window, allowed, score_scale):
    query_f = query_block.astype(jnp.float32)
    grad_f = grad_block.astype(jnp.float32)
    key_f = key_window.astype(jnp.float32)
    value_f = value_window.astype(jnp.float32)
    scores = jnp.einsum('tkgd,skd->kgts', query_f, key_f) * score_scale
    scores = jnp.where(allowed[None, None], scores, -1e30)
    row_max = jnp.max(scores, axis=-1, keepdims=True)
    weights_raw = jnp.exp(scores - row_max)
    prob_full = weights_raw / jnp.sum(weights_raw, axis=-1, keepdims=True)
    grad_p = jnp.einsum('tkgd,skd->kgts', grad_f, value_f)
    row_delta = jnp.sum(prob_full * grad_p, axis=-1, keepdims=True)
    grad_s = (prob_full * (grad_p - row_delta)).astype(jnp.bfloat16)
    grad_s_f = grad_s.astype(jnp.float32)
    grad_q = (jnp.einsum('kgts,skd->tkgd', grad_s_f, key_f) * score_scale).astype(jnp.bfloat16)
    grad_k = jnp.einsum('kgts,tkgd->skd', grad_s_f, query_f) * score_scale
    return grad_q, grad_k


def reference(queries, key_vectors, value_vectors, output_grad, doc_lengths):
    score_scale = HD ** -0.5
    blocks = SEQ // TOK_DEV
    query_blocks = queries.reshape(blocks, TOK_DEV, KVH, GROUP, HD)
    grad_blocks = output_grad.reshape(blocks, TOK_DEV, KVH, GROUP, HD)
    front = jnp.zeros((2 * TOK_DEV, KVH * HD), jnp.bfloat16)
    key_padded = jnp.concatenate([front, key_vectors], axis=0).reshape(SEQ + 2 * TOK_DEV, KVH, HD)
    value_padded = jnp.concatenate([front, value_vectors], axis=0).reshape(SEQ + 2 * TOK_DEV, KVH, HD)
    pending_start = jnp.zeros((2 * TOK_DEV, KVH, HD), jnp.float32)

    def advance(pending, inputs):
        block, query_block, grad_block = inputs
        start = (block * TOK_DEV).astype(jnp.int32)
        key_window = lax.dynamic_slice_in_dim(key_padded, start, 3 * TOK_DEV, 0)
        value_window = lax.dynamic_slice_in_dim(value_padded, start, 3 * TOK_DEV, 0)
        query_pos = start + jnp.arange(TOK_DEV, dtype=jnp.int32)
        key_pos = start - 2 * TOK_DEV + jnp.arange(3 * TOK_DEV, dtype=jnp.int32)
        query_docs = doc_index(doc_lengths, query_pos)
        key_docs = doc_index(doc_lengths, key_pos)
        allowed = (query_docs[:, None] == key_docs[None, :]) & (key_pos[None, :] <= query_pos[:, None])
        grad_q, grad_k = window_grads(query_block, grad_block, key_window, value_window, allowed, score_scale)
        padding = jnp.zeros((TOK_DEV, KVH, HD), jnp.float32)
        total = jnp.concatenate([pending, padding], axis=0) + grad_k
        return total[TOK_DEV:], (grad_q, total[:TOK_DEV])

    pending, (grad_q_all, finished) = lax.scan(
        advance, pending_start, (jnp.arange(blocks, dtype=jnp.int32), query_blocks, grad_blocks))
    finished = finished.reshape(blocks * TOK_DEV, KVH, HD)
    grads = jnp.concatenate([finished[2 * TOK_DEV:], pending], axis=0)
    query_grad = grad_q_all.reshape(SEQ, QH * HD)
    key_grad = grads.reshape(SEQ, KVH * HD).astype(jnp.bfloat16)
    return (query_grad, key_grad)
```

```python
import jax
import jax.numpy as jnp
from jax import lax
from jax.sharding import PartitionSpec as P

QH = 32
KVH = 4
HD = 128
GROUP = 8


def shifted(block, axis, distance):
    devices = range(lax.axis_size(axis))
    route = [(i - distance, i) for i in devices if i - distance in devices]
    return lax.ppermute(block, axis, route)


def doc_index(doc_lengths, positions):
    doc_ends = jnp.cumsum(doc_lengths)
    counted = jnp.sum((positions[:, None] >= doc_ends[None, :]).astype(jnp.int32), axis=1)
    return jnp.where(positions < 0, -1, counted)


def head_grads(query_block, grad_block, key_window, value_window, allowed, score_scale):
    scores = (
        jnp.einsum("tgd,sd->gts", query_block, key_window, preferred_element_type=jnp.float32)
        * score_scale
    )
    scores = jnp.where(allowed[None], scores, -1e30)
    row_max = jnp.max(scores, axis=-1, keepdims=True)
    weights_raw = jnp.exp(scores - row_max)
    prob_full = weights_raw / jnp.sum(weights_raw, axis=-1, keepdims=True)
    grad_p = jnp.einsum("tgd,sd->gts", grad_block, value_window, preferred_element_type=jnp.float32)
    row_delta = jnp.sum(prob_full * grad_p, axis=-1, keepdims=True)
    grad_s = (prob_full * (grad_p - row_delta)).astype(jnp.bfloat16)
    grad_q = (
        jnp.einsum("gts,sd->tgd", grad_s, key_window, preferred_element_type=jnp.float32)
        * score_scale
    )
    grad_k = (
        jnp.einsum("gts,tgd->sd", grad_s, query_block, preferred_element_type=jnp.float32)
        * score_scale
    )
    return (grad_q.astype(jnp.bfloat16), grad_k)


def allowed_pairs(doc_lengths, query_pos, key_pos):
    query_docs = doc_index(doc_lengths, query_pos)
    key_docs = doc_index(doc_lengths, key_pos)
    return (query_docs[:, None] == key_docs[None, :]) & (key_pos[None, :] <= query_pos[:, None])


def fetch_rim(key_value, places):
    return shifted(key_value, ("ctx", "uly"), places)


def send_back(partial_grads, places):
    return shifted(partial_grads, ("ctx", "uly"), places)


def body(queries, key_vectors, value_vectors, output_grad, doc_lengths):
    block_rows = queries.shape[0]
    score_scale = HD ** (-0.5)
    key_value = jnp.stack([key_vectors, value_vectors])
    device_index = lax.axis_index(("ctx", "uly"))
    near_rim = fetch_rim(key_value, 1)
    far_rim = fetch_rim(near_rim, 1)
    window = jnp.concatenate([far_rim, near_rim, key_value], axis=1)
    window_heads = jnp.transpose(window.reshape(2, 3 * block_rows, KVH, HD), (0, 2, 1, 3))
    query_heads = jnp.transpose(queries.reshape(block_rows, KVH, GROUP, HD), (1, 0, 2, 3))
    grad_heads = jnp.transpose(output_grad.reshape(block_rows, KVH, GROUP, HD), (1, 0, 2, 3))
    query_pos = device_index * block_rows + jnp.arange(block_rows, dtype=jnp.int32)
    key_pos = (
        device_index * block_rows - 2 * block_rows + jnp.arange(3 * block_rows, dtype=jnp.int32)
    )
    allowed = allowed_pairs(doc_lengths, query_pos, key_pos)

    def per_head(head_item):
        return head_grads(
            head_item[0], head_item[1], head_item[2], head_item[3], allowed, score_scale
        )

    grad_q, grad_k = lax.map(per_head, (query_heads, grad_heads, window_heads[0], window_heads[1]))
    query_grad = jnp.transpose(grad_q, (1, 0, 2, 3)).reshape(block_rows, QH * HD)
    window_grad = jnp.transpose(grad_k, (1, 0, 2)).reshape(3 * block_rows, KVH * HD)
    relayed = send_back(window_grad[:block_rows].astype(jnp.bfloat16), -1)
    near_sum = window_grad[block_rows : 2 * block_rows] + relayed.astype(jnp.float32)
    arrived = send_back(near_sum.astype(jnp.bfloat16), -1)
    own_part = window_grad[2 * block_rows :] + arrived.astype(jnp.float32)
    key_grad = own_part.astype(jnp.bfloat16)
    return (query_grad, key_grad)


def solution(mesh):
    placed = (
        P(("dp", "ctx", "uly"), None),
        P(("dp", "ctx", "uly"), None),
        P(("dp", "ctx", "uly"), None),
        P(("dp", "ctx", "uly"), None),
        P("dp"),
    )
    return jax.shard_map(
        body,
        mesh=mesh,
        in_specs=placed,
        out_specs=(P(("dp", "ctx", "uly"), None), P(("dp", "ctx", "uly"), None)),
        check_vma=False,
    )
```

```python
import jax
import jax.numpy as jnp
from jax import lax
from jax.sharding import PartitionSpec as P

QH = 32
KVH = 4
HD = 128
GROUP = 8
NEG = -1e30


def shifted(block, axis, distance):
    devices = range(lax.axis_size(axis))
    route = [(i - distance, i) for i in devices if i - distance in devices]
    return lax.ppermute(block, axis, route)


def doc_index(doc_lengths, positions):
    doc_ends = jnp.cumsum(doc_lengths)
    counted = jnp.sum((positions[:, None] >= doc_ends[None, :]).astype(jnp.int32), axis=1)
    return jnp.where(positions < 0, -1, counted)


def allowed_pairs(doc_lengths, query_pos, key_pos):
    query_docs = doc_index(doc_lengths, query_pos)
    key_docs = doc_index(doc_lengths, key_pos)
    return (query_docs[:, None] == key_docs[None, :]) & (key_pos[None, :] <= query_pos[:, None])


def scores_of(query_heads, key_heads, allowed, score_scale):
    scores = (
        jnp.einsum("tghd,sgd->ghts", query_heads, key_heads, preferred_element_type=jnp.float32)
        * score_scale
    )
    return jnp.where(allowed[None, None], scores, NEG)


def body(queries, key_vectors, value_vectors, output_grad, doc_lengths):
    rows = queries.shape[0]
    score_scale = HD ** (-0.5)
    axes = ("ctx", "uly")
    key_value = jnp.stack([key_vectors, value_vectors])
    near_rim = shifted(key_value, axes, 1)
    far_rim = shifted(key_value, axes, 2)
    device_index = lax.axis_index(axes)
    query_heads = queries.reshape(rows, KVH, GROUP, HD)
    grad_heads = output_grad.reshape(rows, KVH, GROUP, HD)
    own_keys = key_vectors.reshape(rows, KVH, HD)
    own_values = value_vectors.reshape(rows, KVH, HD)
    query_pos = device_index * rows + jnp.arange(rows, dtype=jnp.int32)
    own_pos = query_pos
    rim_pos = device_index * rows - 2 * rows + jnp.arange(2 * rows, dtype=jnp.int32)
    own_allowed = allowed_pairs(doc_lengths, query_pos, own_pos)
    rim_allowed = allowed_pairs(doc_lengths, query_pos, rim_pos)

    own_scores = scores_of(query_heads, own_keys, own_allowed, score_scale)
    own_max = jnp.max(own_scores, axis=-1, keepdims=True)
    own_exp = jnp.exp(own_scores - own_max)
    own_sum = jnp.sum(own_exp, axis=-1, keepdims=True)
    own_grad_p = jnp.einsum(
        "tghd,sgd->ghts", grad_heads, own_values, preferred_element_type=jnp.float32
    )
    own_dot = jnp.sum(own_exp * own_grad_p, axis=-1, keepdims=True)

    rim = jnp.concatenate([far_rim, near_rim], axis=1).reshape(2, 2 * rows, KVH, HD)
    rim_keys, rim_values = rim[0], rim[1]
    rim_scores = scores_of(query_heads, rim_keys, rim_allowed, score_scale)
    row_max = jnp.maximum(own_max, jnp.max(rim_scores, axis=-1, keepdims=True))
    rim_exp = jnp.exp(rim_scores - row_max)
    own_rescale = jnp.exp(own_max - row_max)
    row_sum = own_sum * own_rescale + jnp.sum(rim_exp, axis=-1, keepdims=True)
    rim_grad_p = jnp.einsum(
        "tghd,sgd->ghts", grad_heads, rim_values, preferred_element_type=jnp.float32
    )
    row_delta = (
        own_dot * own_rescale + jnp.sum(rim_exp * rim_grad_p, axis=-1, keepdims=True)
    ) / row_sum
    rim_grad_s = ((rim_exp / row_sum) * (rim_grad_p - row_delta)).astype(jnp.bfloat16)
    rim_key_grad = (
        jnp.einsum("ghts,tghd->sgd", rim_grad_s, query_heads, preferred_element_type=jnp.float32)
        * score_scale
    ).reshape(2 * rows, KVH * HD)
    far_back = shifted(rim_key_grad[:rows].astype(jnp.bfloat16), axes, -2)
    near_back = shifted(rim_key_grad[rows:].astype(jnp.bfloat16), axes, -1)

    own_prob = own_exp * (own_rescale / row_sum)
    own_grad_s = (own_prob * (own_grad_p - row_delta)).astype(jnp.bfloat16)
    own_key_grad = (
        jnp.einsum("ghts,tghd->sgd", own_grad_s, query_heads, preferred_element_type=jnp.float32)
        * score_scale
    ).reshape(rows, KVH * HD)
    query_grad = (
        jnp.einsum("ghts,sgd->tghd", own_grad_s, own_keys, preferred_element_type=jnp.float32)
        + jnp.einsum("ghts,sgd->tghd", rim_grad_s, rim_keys, preferred_element_type=jnp.float32)
    ) * score_scale
    query_grad = query_grad.astype(jnp.bfloat16).reshape(rows, QH * HD)
    key_grad = (
        own_key_grad + near_back.astype(jnp.float32) + far_back.astype(jnp.float32)
    ).astype(jnp.bfloat16)
    return (query_grad, key_grad)


def solution(mesh):
    placed = (
        P(("dp", "ctx", "uly"), None),
        P(("dp", "ctx", "uly"), None),
        P(("dp", "ctx", "uly"), None),
        P(("dp", "ctx", "uly"), None),
        P("dp"),
    )
    return jax.shard_map(
        body,
        mesh=mesh,
        in_specs=placed,
        out_specs=(P(("dp", "ctx", "uly"), None), P(("dp", "ctx", "uly"), None)),
        check_vma=False,
    )
```

```python
import functools

import jax
import jax.numpy as jnp
from jax import lax
from jax.experimental import pallas as pl
from jax.experimental.pallas import tpu as pltpu
from jax.sharding import PartitionSpec as P

QH = 32
KVH = 4
HD = 128
GROUP = 8
NEG = -1e30
SCALE = HD ** (-0.5)


def shifted(block, axis, distance):
    devices = range(lax.axis_size(axis))
    route = [(i - distance, i) for i in devices if i - distance in devices]
    return lax.ppermute(block, axis, route)


def doc_index(doc_lengths, positions):
    doc_ends = jnp.cumsum(doc_lengths)
    counted = jnp.sum((positions[:, None] >= doc_ends[None, :]).astype(jnp.int32), axis=1)
    return jnp.where(positions < 0, -1, counted)


def mask_bias(doc_lengths, query_pos, key_pos):
    query_docs = doc_index(doc_lengths, query_pos)
    key_docs = doc_index(doc_lengths, key_pos)
    allowed = (query_docs[:, None] == key_docs[None, :]) & (key_pos[None, :] <= query_pos[:, None])
    return jnp.where(allowed, 0.0, NEG).astype(jnp.float32)


def q_kt(q, k):
    return lax.dot_general(q, k, (((1,), (1,)), ((), ())), preferred_element_type=jnp.float32)


def st_q(s, q):
    return lax.dot_general(s, q, (((0,), (0,)), ((), ())), preferred_element_type=jnp.float32)


def s_k(s, k):
    return jnp.dot(s, k, preferred_element_type=jnp.float32)


def head_cols(h):
    return slice(h * HD, (h + 1) * HD)


def own_stats_kernel(q_ref, do_ref, k_ref, v_ref, bias_ref, m_ref, l_ref, t_ref):
    k = k_ref[...]
    v = v_ref[...]
    bias = bias_ref[...]
    for h in range(GROUP):
        q = q_ref[:, head_cols(h)]
        do = do_ref[:, head_cols(h)]
        s = q_kt(q, k) * SCALE + bias
        m = jnp.max(s, axis=1, keepdims=True)
        e = jnp.exp(s - m)
        dp = q_kt(do, v)
        m_ref[h] = m
        l_ref[h] = jnp.sum(e, axis=1, keepdims=True)
        t_ref[h] = jnp.sum(e * dp, axis=1, keepdims=True)


def rim_kernel(q_ref, do_ref, far_ref, near_ref, bias_far_ref, bias_near_ref,
               m0_ref, l0_ref, t0_ref,
               dk_far_ref, dk_near_ref, dq_ref, m_ref, il_ref, d_ref):
    kf = far_ref[0]
    vf = far_ref[1]
    kn = near_ref[0]
    vn = near_ref[1]
    bias_far = bias_far_ref[...]
    bias_near = bias_near_ref[...]
    acc_far = jnp.zeros((HD, HD), jnp.float32)
    acc_near = jnp.zeros((HD, HD), jnp.float32)
    for h in range(GROUP):
        q = q_ref[:, head_cols(h)]
        do = do_ref[:, head_cols(h)]
        s_f = q_kt(q, kf) * SCALE + bias_far
        s_n = q_kt(q, kn) * SCALE + bias_near
        m0 = m0_ref[h]
        m = jnp.maximum(
            m0,
            jnp.maximum(jnp.max(s_f, axis=1, keepdims=True), jnp.max(s_n, axis=1, keepdims=True)),
        )
        a = jnp.exp(m0 - m)
        e_f = jnp.exp(s_f - m)
        e_n = jnp.exp(s_n - m)
        dp_f = q_kt(do, vf)
        dp_n = q_kt(do, vn)
        row_sum = (
            l0_ref[h] * a
            + jnp.sum(e_f, axis=1, keepdims=True)
            + jnp.sum(e_n, axis=1, keepdims=True)
        )
        row_dot = (
            t0_ref[h] * a
            + jnp.sum(e_f * dp_f, axis=1, keepdims=True)
            + jnp.sum(e_n * dp_n, axis=1, keepdims=True)
        )
        inv_l = 1.0 / row_sum
        delta = row_dot * inv_l
        ds_f = ((e_f * inv_l) * (dp_f - delta)).astype(jnp.bfloat16)
        ds_n = ((e_n * inv_l) * (dp_n - delta)).astype(jnp.bfloat16)
        acc_far = acc_far + st_q(ds_f, q)
        acc_near = acc_near + st_q(ds_n, q)
        dq_ref[:, head_cols(h)] = s_k(ds_f, kf) + s_k(ds_n, kn)
        m_ref[h] = m
        il_ref[h] = inv_l
        d_ref[h] = delta
    dk_far_ref[...] = (acc_far * SCALE).astype(dk_far_ref.dtype)
    dk_near_ref[...] = (acc_near * SCALE).astype(dk_near_ref.dtype)


def own_grads_kernel(q_ref, do_ref, k_ref, v_ref, bias_ref, m_ref, il_ref, d_ref, dq_rim_ref,
                     dq_ref, dk_ref):
    k = k_ref[...]
    v = v_ref[...]
    bias = bias_ref[...]
    acc = jnp.zeros((HD, HD), jnp.float32)
    for h in range(GROUP):
        q = q_ref[:, head_cols(h)]
        do = do_ref[:, head_cols(h)]
        s = q_kt(q, k) * SCALE + bias
        p = jnp.exp(s - m_ref[h]) * il_ref[h]
        dp = q_kt(do, v)
        ds = (p * (dp - d_ref[h])).astype(jnp.bfloat16)
        acc = acc + st_q(ds, q)
        dq = (s_k(ds, k) + dq_rim_ref[:, head_cols(h)]) * SCALE
        dq_ref[:, head_cols(h)] = dq.astype(dq_ref.dtype)
    dk_ref[...] = acc * SCALE


def heads_spec(rows):
    return pl.BlockSpec((rows, GROUP * HD), lambda g: (0, g))


def kv_spec(rows):
    return pl.BlockSpec((rows, HD), lambda g: (0, g))


def stacked_spec(rows):
    return pl.BlockSpec((2, rows, HD), lambda g: (0, 0, g))


def full_spec(shape):
    return pl.BlockSpec(shape, lambda g: (0,) * len(shape))


def stat_spec(rows):
    return pl.BlockSpec((GROUP, rows, 1), lambda g: (g, 0, 0))


def params():
    return pltpu.CompilerParams(dimension_semantics=("arbitrary",))


def cost(rows, matmuls, exps):
    flops = 2 * rows * rows * HD * QH * matmuls
    return pl.CostEstimate(
        flops=flops, transcendentals=rows * rows * QH * exps, bytes_accessed=4 * rows * QH * HD * 2
    )


def own_stats(queries, output_grad, keys, values, bias):
    rows = queries.shape[0]
    stat = jax.ShapeDtypeStruct((QH, rows, 1), jnp.float32)
    return pl.pallas_call(
        own_stats_kernel,
        grid=(KVH,),
        in_specs=[heads_spec(rows), heads_spec(rows), kv_spec(rows), kv_spec(rows),
                  full_spec((rows, rows))],
        out_specs=[stat_spec(rows)] * 3,
        out_shape=[stat] * 3,
        compiler_params=params(),
        cost_estimate=cost(rows, 2, 1),
    )(queries, output_grad, keys, values, bias)


def rim_grads(queries, output_grad, far, near, bias_far, bias_near, m0, l0, t0):
    rows = queries.shape[0]
    stat = jax.ShapeDtypeStruct((QH, rows, 1), jnp.float32)
    part = jax.ShapeDtypeStruct((rows, KVH * HD), jnp.bfloat16)
    return pl.pallas_call(
        rim_kernel,
        grid=(KVH,),
        in_specs=[heads_spec(rows), heads_spec(rows), stacked_spec(rows), stacked_spec(rows),
                  full_spec((rows, rows)), full_spec((rows, rows))]
        + [stat_spec(rows)] * 3,
        out_specs=[kv_spec(rows), kv_spec(rows), heads_spec(rows)] + [stat_spec(rows)] * 3,
        out_shape=[part, part, jax.ShapeDtypeStruct((rows, QH * HD), jnp.float32)] + [stat] * 3,
        compiler_params=params(),
        cost_estimate=cost(rows, 8, 2),
    )(queries, output_grad, far, near, bias_far, bias_near, m0, l0, t0)


def own_grads(queries, output_grad, keys, values, bias, m, il, d, dq_rim):
    rows = queries.shape[0]
    return pl.pallas_call(
        own_grads_kernel,
        grid=(KVH,),
        in_specs=[heads_spec(rows), heads_spec(rows), kv_spec(rows), kv_spec(rows),
                  full_spec((rows, rows))]
        + [stat_spec(rows)] * 3
        + [heads_spec(rows)],
        out_specs=[heads_spec(rows), kv_spec(rows)],
        out_shape=[jax.ShapeDtypeStruct((rows, QH * HD), jnp.bfloat16),
                   jax.ShapeDtypeStruct((rows, KVH * HD), jnp.float32)],
        compiler_params=params(),
        cost_estimate=cost(rows, 4, 1),
    )(queries, output_grad, keys, values, bias, m, il, d, dq_rim)


def body(queries, key_vectors, value_vectors, output_grad, doc_lengths):
    rows = queries.shape[0]
    axes = ("ctx", "uly")
    key_value = jnp.stack([key_vectors, value_vectors])
    near_rim = shifted(key_value, axes, 1)
    far_rim = shifted(key_value, axes, 2)
    device_index = lax.axis_index(axes)
    base = device_index * rows
    query_pos = base + jnp.arange(rows, dtype=jnp.int32)
    bias_own = mask_bias(doc_lengths, query_pos, query_pos)
    bias_near = mask_bias(doc_lengths, query_pos, query_pos - rows)
    bias_far = mask_bias(doc_lengths, query_pos, query_pos - 2 * rows)

    m0, l0, t0 = own_stats(queries, output_grad, key_vectors, value_vectors, bias_own)
    dk_far, dk_near, dq_rim, m, il, d = rim_grads(
        queries, output_grad, far_rim, near_rim, bias_far, bias_near, m0, l0, t0
    )
    far_back = shifted(dk_far, axes, -2)
    near_back = shifted(dk_near, axes, -1)
    query_grad, own_key_grad = own_grads(
        queries, output_grad, key_vectors, value_vectors, bias_own, m, il, d, dq_rim
    )
    key_grad = (
        own_key_grad + near_back.astype(jnp.float32) + far_back.astype(jnp.float32)
    ).astype(jnp.bfloat16)
    return (query_grad, key_grad)


def solution(mesh):
    placed = (
        P(("dp", "ctx", "uly"), None),
        P(("dp", "ctx", "uly"), None),
        P(("dp", "ctx", "uly"), None),
        P(("dp", "ctx", "uly"), None),
        P("dp"),
    )
    return jax.shard_map(
        body,
        mesh=mesh,
        in_specs=placed,
        out_specs=(P(("dp", "ctx", "uly"), None), P(("dp", "ctx", "uly"), None)),
        check_vma=False,
    )
```

```python
import jax
import jax.numpy as jnp
from jax import lax
from jax.sharding import PartitionSpec as P

QH = 32
KVH = 4
HD = 128
GROUP = 8
NEG = -1e30


def shifted(block, axis, distance):
    devices = range(lax.axis_size(axis))
    route = [(i - distance, i) for i in devices if i - distance in devices]
    return lax.ppermute(block, axis, route)


def doc_index(doc_lengths, positions):
    doc_ends = jnp.cumsum(doc_lengths)
    counted = jnp.sum((positions[:, None] >= doc_ends[None, :]).astype(jnp.int32), axis=1)
    return jnp.where(positions < 0, -1, counted)


def allowed_pairs(doc_lengths, query_pos, key_pos):
    query_docs = doc_index(doc_lengths, query_pos)
    key_docs = doc_index(doc_lengths, key_pos)
    return (query_docs[:, None] == key_docs[None, :]) & (key_pos[None, :] <= query_pos[:, None])


def scores_of(query_heads, key_heads, allowed, score_scale):
    scores = (
        jnp.einsum("tghd,sgd->ghts", query_heads, key_heads, preferred_element_type=jnp.float32)
        * score_scale
    )
    return jnp.where(allowed[None, None], scores, NEG)


def fetch_rims(key_value):
    width = lax.axis_size("uly")
    groups = lax.axis_size("ctx")
    place = lax.axis_index("uly")
    gathered = lax.all_gather(key_value, "uly")
    tail = gathered[width - 2 :]
    route = [
        ((group - 1) * width + spot, group * width + spot)
        for group in range(1, groups)
        for spot in (0, 1)
    ]
    wrap = lax.ppermute(tail, ("ctx", "uly"), route)
    before_one = lax.dynamic_index_in_dim(gathered, jnp.maximum(place - 1, 0), 0, keepdims=False)
    before_two = lax.dynamic_index_in_dim(gathered, jnp.maximum(place - 2, 0), 0, keepdims=False)
    near_rim = jnp.where(place >= 1, before_one, wrap[1])
    far_rim = jnp.where(place >= 2, before_two, jnp.where(place == 1, wrap[1], wrap[0]))
    return near_rim, far_rim


def body(queries, key_vectors, value_vectors, output_grad, doc_lengths):
    rows = queries.shape[0]
    score_scale = HD ** (-0.5)
    axes = ("ctx", "uly")
    key_value = jnp.stack([key_vectors, value_vectors])
    near_rim, far_rim = fetch_rims(key_value)
    device_index = lax.axis_index(axes)
    query_heads = queries.reshape(rows, KVH, GROUP, HD)
    grad_heads = output_grad.reshape(rows, KVH, GROUP, HD)
    own_keys = key_vectors.reshape(rows, KVH, HD)
    own_values = value_vectors.reshape(rows, KVH, HD)
    query_pos = device_index * rows + jnp.arange(rows, dtype=jnp.int32)
    own_pos = query_pos
    rim_pos = device_index * rows - 2 * rows + jnp.arange(2 * rows, dtype=jnp.int32)
    own_allowed = allowed_pairs(doc_lengths, query_pos, own_pos)
    rim_allowed = allowed_pairs(doc_lengths, query_pos, rim_pos)

    own_scores = scores_of(query_heads, own_keys, own_allowed, score_scale)
    own_max = jnp.max(own_scores, axis=-1, keepdims=True)
    own_exp = jnp.exp(own_scores - own_max)
    own_sum = jnp.sum(own_exp, axis=-1, keepdims=True)
    own_grad_p = jnp.einsum(
        "tghd,sgd->ghts", grad_heads, own_values, preferred_element_type=jnp.float32
    )
    own_dot = jnp.sum(own_exp * own_grad_p, axis=-1, keepdims=True)

    rim = jnp.concatenate([far_rim, near_rim], axis=1).reshape(2, 2 * rows, KVH, HD)
    rim_keys, rim_values = rim[0], rim[1]
    rim_scores = scores_of(query_heads, rim_keys, rim_allowed, score_scale)
    row_max = jnp.maximum(own_max, jnp.max(rim_scores, axis=-1, keepdims=True))
    rim_exp = jnp.exp(rim_scores - row_max)
    own_rescale = jnp.exp(own_max - row_max)
    row_sum = own_sum * own_rescale + jnp.sum(rim_exp, axis=-1, keepdims=True)
    rim_grad_p = jnp.einsum(
        "tghd,sgd->ghts", grad_heads, rim_values, preferred_element_type=jnp.float32
    )
    row_delta = (
        own_dot * own_rescale + jnp.sum(rim_exp * rim_grad_p, axis=-1, keepdims=True)
    ) / row_sum
    rim_grad_s = ((rim_exp / row_sum) * (rim_grad_p - row_delta)).astype(jnp.bfloat16)
    rim_key_grad = (
        jnp.einsum("ghts,tghd->sgd", rim_grad_s, query_heads, preferred_element_type=jnp.float32)
        * score_scale
    ).reshape(2 * rows, KVH * HD)
    far_back = shifted(rim_key_grad[:rows].astype(jnp.bfloat16), axes, -2)
    near_back = shifted(rim_key_grad[rows:].astype(jnp.bfloat16), axes, -1)

    own_prob = own_exp * (own_rescale / row_sum)
    own_grad_s = (own_prob * (own_grad_p - row_delta)).astype(jnp.bfloat16)
    own_key_grad = (
        jnp.einsum("ghts,tghd->sgd", own_grad_s, query_heads, preferred_element_type=jnp.float32)
        * score_scale
    ).reshape(rows, KVH * HD)
    query_grad = (
        jnp.einsum("ghts,sgd->tghd", own_grad_s, own_keys, preferred_element_type=jnp.float32)
        + jnp.einsum("ghts,sgd->tghd", rim_grad_s, rim_keys, preferred_element_type=jnp.float32)
    ) * score_scale
    query_grad = query_grad.astype(jnp.bfloat16).reshape(rows, QH * HD)
    key_grad = (
        own_key_grad + near_back.astype(jnp.float32) + far_back.astype(jnp.float32)
    ).astype(jnp.bfloat16)
    return (query_grad, key_grad)


def solution(mesh):
    placed = (
        P(("dp", "ctx", "uly"), None),
        P(("dp", "ctx", "uly"), None),
        P(("dp", "ctx", "uly"), None),
        P(("dp", "ctx", "uly"), None),
        P("dp"),
    )
    return jax.shard_map(
        body,
        mesh=mesh,
        in_specs=placed,
        out_specs=(P(("dp", "ctx", "uly"), None), P(("dp", "ctx", "uly"), None)),
        check_vma=False,
    )
```

```python
import jax
import jax.numpy as jnp
from jax import lax
from jax.sharding import PartitionSpec as P

QH = 32
KVH = 4
HD = 128
GROUP = 8
NEG = -1e30


def shifted(block, axis, distance):
    devices = range(lax.axis_size(axis))
    route = [(i - distance, i) for i in devices if i - distance in devices]
    return lax.ppermute(block, axis, route)


def doc_index(doc_lengths, positions):
    doc_ends = jnp.cumsum(doc_lengths)
    counted = jnp.sum((positions[:, None] >= doc_ends[None, :]).astype(jnp.int32), axis=1)
    return jnp.where(positions < 0, -1, counted)


def allowed_pairs(doc_lengths, query_pos, key_pos):
    query_docs = doc_index(doc_lengths, query_pos)
    key_docs = doc_index(doc_lengths, key_pos)
    return (query_docs[:, None] == key_docs[None, :]) & (key_pos[None, :] <= query_pos[:, None])


def scores_of(query_heads, key_heads, allowed, score_scale):
    scores = (
        jnp.einsum("tghd,sgd->ghts", query_heads, key_heads, preferred_element_type=jnp.float32)
        * score_scale
    )
    return jnp.where(allowed[None, None], scores, NEG)


def key_grad_of(grad_s, query_heads, score_scale):
    return (
        jnp.einsum("ghts,tghd->gsd", grad_s, query_heads, preferred_element_type=jnp.float32)
        * score_scale
    )


def query_grad_of(grad_s, keys):
    return jnp.einsum("ghts,sgd->ghtd", grad_s, keys, preferred_element_type=jnp.float32)


def body(queries, key_vectors, value_vectors, output_grad, doc_lengths):
    rows = queries.shape[0]
    score_scale = HD ** (-0.5)
    axes = ("ctx", "uly")
    key_value = jnp.stack([key_vectors, value_vectors])
    near_rim = shifted(key_value, axes, 1)
    far_rim = shifted(key_value, axes, 2)
    device_index = lax.axis_index(axes)
    query_heads = queries.reshape(rows, KVH, GROUP, HD)
    grad_heads = output_grad.reshape(rows, KVH, GROUP, HD)
    own_keys = key_vectors.reshape(rows, KVH, HD)
    own_values = value_vectors.reshape(rows, KVH, HD)
    query_pos = device_index * rows + jnp.arange(rows, dtype=jnp.int32)
    own_pos = query_pos
    own_allowed = allowed_pairs(doc_lengths, query_pos, own_pos)
    near_allowed = allowed_pairs(doc_lengths, query_pos, own_pos - rows)
    far_allowed = allowed_pairs(doc_lengths, query_pos, own_pos - 2 * rows)

    own_scores = scores_of(query_heads, own_keys, own_allowed, score_scale)
    own_max = jnp.max(own_scores, axis=-1, keepdims=True)
    own_exp = jnp.exp(own_scores - own_max)
    own_sum = jnp.sum(own_exp, axis=-1, keepdims=True)
    own_grad_p = jnp.einsum(
        "tghd,sgd->ghts", grad_heads, own_values, preferred_element_type=jnp.float32
    )
    own_dot = jnp.sum(own_exp * own_grad_p, axis=-1, keepdims=True)

    far_keys = far_rim[0].reshape(rows, KVH, HD)
    far_values = far_rim[1].reshape(rows, KVH, HD)
    near_keys = near_rim[0].reshape(rows, KVH, HD)
    near_values = near_rim[1].reshape(rows, KVH, HD)
    far_scores = scores_of(query_heads, far_keys, far_allowed, score_scale)
    near_scores = scores_of(query_heads, near_keys, near_allowed, score_scale)
    row_max = jnp.maximum(
        own_max,
        jnp.maximum(
            jnp.max(far_scores, axis=-1, keepdims=True),
            jnp.max(near_scores, axis=-1, keepdims=True),
        ),
    )
    far_exp = jnp.exp(far_scores - row_max)
    near_exp = jnp.exp(near_scores - row_max)
    own_rescale = jnp.exp(own_max - row_max)
    row_sum = (
        own_sum * own_rescale
        + jnp.sum(far_exp, axis=-1, keepdims=True)
        + jnp.sum(near_exp, axis=-1, keepdims=True)
    )
    far_grad_p = jnp.einsum(
        "tghd,sgd->ghts", grad_heads, far_values, preferred_element_type=jnp.float32
    )
    near_grad_p = jnp.einsum(
        "tghd,sgd->ghts", grad_heads, near_values, preferred_element_type=jnp.float32
    )
    row_delta = (
        own_dot * own_rescale
        + jnp.sum(far_exp * far_grad_p, axis=-1, keepdims=True)
        + jnp.sum(near_exp * near_grad_p, axis=-1, keepdims=True)
    ) / row_sum
    far_grad_s = ((far_exp / row_sum) * (far_grad_p - row_delta)).astype(jnp.bfloat16)
    near_grad_s = ((near_exp / row_sum) * (near_grad_p - row_delta)).astype(jnp.bfloat16)
    far_key_grad = key_grad_of(far_grad_s, query_heads, score_scale)
    near_key_grad = key_grad_of(near_grad_s, query_heads, score_scale)
    far_back = shifted(far_key_grad.astype(jnp.bfloat16), axes, -2)
    near_back = shifted(near_key_grad.astype(jnp.bfloat16), axes, -1)

    own_prob = own_exp * (own_rescale / row_sum)
    own_grad_s = (own_prob * (own_grad_p - row_delta)).astype(jnp.bfloat16)
    own_key_grad = key_grad_of(own_grad_s, query_heads, score_scale)
    query_grad = (
        query_grad_of(own_grad_s, own_keys)
        + query_grad_of(far_grad_s, far_keys)
        + query_grad_of(near_grad_s, near_keys)
    ) * score_scale
    query_grad = jnp.transpose(query_grad.astype(jnp.bfloat16), (2, 0, 1, 3)).reshape(rows, QH * HD)
    key_grad = own_key_grad + near_back.astype(jnp.float32) + far_back.astype(jnp.float32)
    key_grad = jnp.transpose(key_grad, (1, 0, 2)).reshape(rows, KVH * HD).astype(jnp.bfloat16)
    return (query_grad, key_grad)


def solution(mesh):
    placed = (
        P(("dp", "ctx", "uly"), None),
        P(("dp", "ctx", "uly"), None),
        P(("dp", "ctx", "uly"), None),
        P(("dp", "ctx", "uly"), None),
        P("dp"),
    )
    return jax.shard_map(
        body,
        mesh=mesh,
        in_specs=placed,
        out_specs=(P(("dp", "ctx", "uly"), None), P(("dp", "ctx", "uly"), None)),
        check_vma=False,
    )
```

```python
import jax
import jax.numpy as jnp
from jax import lax
from jax.sharding import PartitionSpec as P

QH = 32
KVH = 4
HD = 128
GROUP = 8
NEG = -1e30
PARTS = 2


def shifted(block, axis, distance):
    devices = range(lax.axis_size(axis))
    route = [(i - distance, i) for i in devices if i - distance in devices]
    return lax.ppermute(block, axis, route)


def doc_index(doc_lengths, positions):
    doc_ends = jnp.cumsum(doc_lengths)
    counted = jnp.sum((positions[:, None] >= doc_ends[None, :]).astype(jnp.int32), axis=1)
    return jnp.where(positions < 0, -1, counted)


def allowed_pairs(doc_lengths, query_pos, key_pos):
    query_docs = doc_index(doc_lengths, query_pos)
    key_docs = doc_index(doc_lengths, key_pos)
    return (query_docs[:, None] == key_docs[None, :]) & (key_pos[None, :] <= query_pos[:, None])


def scores_of(query_heads, key_heads, allowed, score_scale):
    scores = (
        jnp.einsum("tghd,sgd->ghts", query_heads, key_heads, preferred_element_type=jnp.float32)
        * score_scale
    )
    return jnp.where(allowed[None, None], scores, NEG)


def grad_p_of(grad_heads, values):
    return jnp.einsum("tghd,sgd->ghts", grad_heads, values, preferred_element_type=jnp.float32)


def key_grad_of(grad_s, query_heads, score_scale):
    return (
        jnp.einsum("ghts,tghd->gsd", grad_s, query_heads, preferred_element_type=jnp.float32)
        * score_scale
    )


def query_grad_of(grad_s, keys):
    return jnp.einsum("ghts,sgd->ghtd", grad_s, keys, preferred_element_type=jnp.float32)


def own_stats(query_heads, grad_heads, own_keys, own_values, own_allowed, score_scale):
    own_scores = scores_of(query_heads, own_keys, own_allowed, score_scale)
    own_max = jnp.max(own_scores, axis=-1, keepdims=True)
    own_exp = jnp.exp(own_scores - own_max)
    own_sum = jnp.sum(own_exp, axis=-1, keepdims=True)
    own_grad_p = grad_p_of(grad_heads, own_values)
    own_dot = jnp.sum(own_exp * own_grad_p, axis=-1, keepdims=True)
    return own_max, own_exp, own_sum, own_grad_p, own_dot


def rim_grads(query_heads, grad_heads, far_rim, near_rim, far_allowed, near_allowed, stats,
              score_scale, rows, heads):
    own_max, own_exp, own_sum, own_grad_p, own_dot = stats
    far_keys = far_rim[0].reshape(rows, heads, HD)
    far_values = far_rim[1].reshape(rows, heads, HD)
    near_keys = near_rim[0].reshape(rows, heads, HD)
    near_values = near_rim[1].reshape(rows, heads, HD)
    far_scores = scores_of(query_heads, far_keys, far_allowed, score_scale)
    near_scores = scores_of(query_heads, near_keys, near_allowed, score_scale)
    row_max = jnp.maximum(
        own_max,
        jnp.maximum(
            jnp.max(far_scores, axis=-1, keepdims=True),
            jnp.max(near_scores, axis=-1, keepdims=True),
        ),
    )
    far_exp = jnp.exp(far_scores - row_max)
    near_exp = jnp.exp(near_scores - row_max)
    own_rescale = jnp.exp(own_max - row_max)
    row_sum = (
        own_sum * own_rescale
        + jnp.sum(far_exp, axis=-1, keepdims=True)
        + jnp.sum(near_exp, axis=-1, keepdims=True)
    )
    far_grad_p = grad_p_of(grad_heads, far_values)
    near_grad_p = grad_p_of(grad_heads, near_values)
    row_delta = (
        own_dot * own_rescale
        + jnp.sum(far_exp * far_grad_p, axis=-1, keepdims=True)
        + jnp.sum(near_exp * near_grad_p, axis=-1, keepdims=True)
    ) / row_sum
    far_grad_s = ((far_exp / row_sum) * (far_grad_p - row_delta)).astype(jnp.bfloat16)
    near_grad_s = ((near_exp / row_sum) * (near_grad_p - row_delta)).astype(jnp.bfloat16)
    far_key_grad = key_grad_of(far_grad_s, query_heads, score_scale).astype(jnp.bfloat16)
    near_key_grad = key_grad_of(near_grad_s, query_heads, score_scale).astype(jnp.bfloat16)
    rim_query_grad = query_grad_of(far_grad_s, far_keys) + query_grad_of(near_grad_s, near_keys)
    return far_key_grad, near_key_grad, rim_query_grad, own_rescale / row_sum, row_delta


def own_grads(query_heads, own_keys, stats, scale_row, row_delta, rim_query_grad, score_scale):
    own_max, own_exp, own_sum, own_grad_p, own_dot = stats
    own_prob = own_exp * scale_row
    own_grad_s = (own_prob * (own_grad_p - row_delta)).astype(jnp.bfloat16)
    own_key_grad = key_grad_of(own_grad_s, query_heads, score_scale)
    query_grad = (query_grad_of(own_grad_s, own_keys) + rim_query_grad) * score_scale
    return query_grad.astype(jnp.bfloat16), own_key_grad


def body(queries, key_vectors, value_vectors, output_grad, doc_lengths):
    rows = queries.shape[0]
    score_scale = HD ** (-0.5)
    axes = ("ctx", "uly")
    heads = KVH // PARTS
    width = heads * HD
    key_value = jnp.stack([key_vectors, value_vectors])
    rims = []
    for part in range(PARTS):
        kv_part = key_value[:, :, part * width : (part + 1) * width]
        rims.append((shifted(kv_part, axes, 1), shifted(kv_part, axes, 2)))
    device_index = lax.axis_index(axes)
    query_pos = device_index * rows + jnp.arange(rows, dtype=jnp.int32)
    own_allowed = allowed_pairs(doc_lengths, query_pos, query_pos)
    near_allowed = allowed_pairs(doc_lengths, query_pos, query_pos - rows)
    far_allowed = allowed_pairs(doc_lengths, query_pos, query_pos - 2 * rows)
    query_heads = queries.reshape(rows, KVH, GROUP, HD)
    grad_heads = output_grad.reshape(rows, KVH, GROUP, HD)
    own_keys = key_vectors.reshape(rows, KVH, HD)
    own_values = value_vectors.reshape(rows, KVH, HD)

    query_parts, key_parts = [], []
    for part in range(PARTS):
        pick = slice(part * heads, (part + 1) * heads)
        q_part = query_heads[:, pick]
        g_part = grad_heads[:, pick]
        k_part = own_keys[:, pick]
        stats = own_stats(q_part, g_part, k_part, own_values[:, pick], own_allowed, score_scale)
        near_rim, far_rim = rims[part]
        far_kg, near_kg, rim_qg, scale_row, row_delta = rim_grads(
            q_part, g_part, far_rim, near_rim, far_allowed, near_allowed, stats,
            score_scale, rows, heads,
        )
        far_back = shifted(far_kg, axes, -2)
        near_back = shifted(near_kg, axes, -1)
        query_grad, own_kg = own_grads(
            q_part, k_part, stats, scale_row, row_delta, rim_qg, score_scale
        )
        query_parts.append(query_grad)
        key_parts.append(own_kg + near_back.astype(jnp.float32) + far_back.astype(jnp.float32))
    query_grad = jnp.concatenate(query_parts, axis=0)
    query_grad = jnp.transpose(query_grad, (2, 0, 1, 3)).reshape(rows, QH * HD)
    key_grad = jnp.concatenate(key_parts, axis=0)
    key_grad = jnp.transpose(key_grad, (1, 0, 2)).reshape(rows, KVH * HD).astype(jnp.bfloat16)
    return (query_grad, key_grad)


def solution(mesh):
    placed = (
        P(("dp", "ctx", "uly"), None),
        P(("dp", "ctx", "uly"), None),
        P(("dp", "ctx", "uly"), None),
        P(("dp", "ctx", "uly"), None),
        P("dp"),
    )
    return jax.shard_map(
        body,
        mesh=mesh,
        in_specs=placed,
        out_specs=(P(("dp", "ctx", "uly"), None), P(("dp", "ctx", "uly"), None)),
        check_vma=False,
    )
```

```python
import jax
import jax.numpy as jnp
from jax import lax
from jax.sharding import PartitionSpec as P

QH = 32
KVH = 4
HD = 128
GROUP = 8
NEG = -1e30


def shifted(block, axis, distance):
    devices = range(lax.axis_size(axis))
    route = [(i - distance, i) for i in devices if i - distance in devices]
    return lax.ppermute(block, axis, route)


def doc_index(doc_lengths, positions):
    doc_ends = jnp.cumsum(doc_lengths)
    counted = jnp.sum((positions[:, None] >= doc_ends[None, :]).astype(jnp.int32), axis=1)
    return jnp.where(positions < 0, -1, counted)


def allowed_pairs(doc_lengths, query_pos, key_pos):
    query_docs = doc_index(doc_lengths, query_pos)
    key_docs = doc_index(doc_lengths, key_pos)
    return (query_docs[:, None] == key_docs[None, :]) & (key_pos[None, :] <= query_pos[:, None])


def scores_of(query_heads, key_heads, allowed, score_scale):
    scores = (
        jnp.einsum("tghd,sgd->ghts", query_heads, key_heads, preferred_element_type=jnp.float32)
        * score_scale
    )
    return jnp.where(allowed[None, None], scores, NEG)


def key_grad_of(grad_s, query_heads, score_scale):
    return (
        jnp.einsum("ghts,tghd->gsd", grad_s, query_heads, preferred_element_type=jnp.float32)
        * score_scale
    )


def query_grad_of(grad_s, keys):
    return jnp.einsum("ghts,sgd->ghtd", grad_s, keys, preferred_element_type=jnp.float32)


def block_stats(query_heads, grad_heads, keys, values, allowed, score_scale):
    scores = scores_of(query_heads, keys, allowed, score_scale)
    block_max = jnp.max(scores, axis=-1, keepdims=True)
    block_exp = jnp.exp(scores - block_max)
    block_sum = jnp.sum(block_exp, axis=-1, keepdims=True)
    grad_p = jnp.einsum("tghd,sgd->ghts", grad_heads, values, preferred_element_type=jnp.float32)
    block_dot = jnp.sum(block_exp * grad_p, axis=-1, keepdims=True)
    return block_max, block_exp, block_sum, grad_p, block_dot


def body(queries, key_vectors, value_vectors, output_grad, doc_lengths):
    rows = queries.shape[0]
    score_scale = HD ** (-0.5)
    axes = ("ctx", "uly")
    key_value = jnp.stack([key_vectors, value_vectors])
    near_rim = shifted(key_value, axes, 1)
    far_rim = shifted(key_value, axes, 2)
    device_index = lax.axis_index(axes)
    query_heads = queries.reshape(rows, KVH, GROUP, HD)
    grad_heads = output_grad.reshape(rows, KVH, GROUP, HD)
    own_keys = key_vectors.reshape(rows, KVH, HD)
    own_values = value_vectors.reshape(rows, KVH, HD)
    query_pos = device_index * rows + jnp.arange(rows, dtype=jnp.int32)
    own_pos = query_pos
    own_allowed = allowed_pairs(doc_lengths, query_pos, own_pos)
    near_allowed = allowed_pairs(doc_lengths, query_pos, own_pos - rows)
    far_allowed = allowed_pairs(doc_lengths, query_pos, own_pos - 2 * rows)

    own_max, own_exp, own_sum, own_grad_p, own_dot = block_stats(
        query_heads, grad_heads, own_keys, own_values, own_allowed, score_scale
    )
    near_keys = near_rim[0].reshape(rows, KVH, HD)
    near_values = near_rim[1].reshape(rows, KVH, HD)
    near_max, near_exp, near_sum, near_grad_p, near_dot = block_stats(
        query_heads, grad_heads, near_keys, near_values, near_allowed, score_scale
    )
    ready, far_rim = lax.optimization_barrier(
        ((own_max, own_exp, own_sum, own_grad_p, own_dot,
          near_max, near_exp, near_sum, near_grad_p, near_dot), far_rim)
    )
    (own_max, own_exp, own_sum, own_grad_p, own_dot,
     near_max, near_exp, near_sum, near_grad_p, near_dot) = ready

    far_keys = far_rim[0].reshape(rows, KVH, HD)
    far_values = far_rim[1].reshape(rows, KVH, HD)
    far_scores = scores_of(query_heads, far_keys, far_allowed, score_scale)
    row_max = jnp.maximum(
        jnp.maximum(own_max, near_max), jnp.max(far_scores, axis=-1, keepdims=True)
    )
    far_exp = jnp.exp(far_scores - row_max)
    own_rescale = jnp.exp(own_max - row_max)
    near_rescale = jnp.exp(near_max - row_max)
    row_sum = (
        own_sum * own_rescale
        + near_sum * near_rescale
        + jnp.sum(far_exp, axis=-1, keepdims=True)
    )
    far_grad_p = jnp.einsum(
        "tghd,sgd->ghts", grad_heads, far_values, preferred_element_type=jnp.float32
    )
    row_delta = (
        own_dot * own_rescale
        + near_dot * near_rescale
        + jnp.sum(far_exp * far_grad_p, axis=-1, keepdims=True)
    ) / row_sum
    near_exp = near_exp * near_rescale
    far_grad_s = ((far_exp / row_sum) * (far_grad_p - row_delta)).astype(jnp.bfloat16)
    near_grad_s = ((near_exp / row_sum) * (near_grad_p - row_delta)).astype(jnp.bfloat16)
    far_key_grad = key_grad_of(far_grad_s, query_heads, score_scale)
    near_key_grad = key_grad_of(near_grad_s, query_heads, score_scale)
    far_back = shifted(far_key_grad.astype(jnp.bfloat16), axes, -2)
    near_back = shifted(near_key_grad.astype(jnp.bfloat16), axes, -1)

    own_prob = own_exp * (own_rescale / row_sum)
    own_grad_s = (own_prob * (own_grad_p - row_delta)).astype(jnp.bfloat16)
    own_key_grad = key_grad_of(own_grad_s, query_heads, score_scale)
    query_grad = (
        query_grad_of(own_grad_s, own_keys)
        + query_grad_of(far_grad_s, far_keys)
        + query_grad_of(near_grad_s, near_keys)
    ) * score_scale
    query_grad = jnp.transpose(query_grad.astype(jnp.bfloat16), (2, 0, 1, 3)).reshape(rows, QH * HD)
    key_grad = own_key_grad + near_back.astype(jnp.float32) + far_back.astype(jnp.float32)
    key_grad = jnp.transpose(key_grad, (1, 0, 2)).reshape(rows, KVH * HD).astype(jnp.bfloat16)
    return (query_grad, key_grad)


def solution(mesh):
    placed = (
        P(("dp", "ctx", "uly"), None),
        P(("dp", "ctx", "uly"), None),
        P(("dp", "ctx", "uly"), None),
        P(("dp", "ctx", "uly"), None),
        P("dp"),
    )
    return jax.shard_map(
        body,
        mesh=mesh,
        in_specs=placed,
        out_specs=(P(("dp", "ctx", "uly"), None), P(("dp", "ctx", "uly"), None)),
        check_vma=False,
    )
```

```python
import jax
import jax.numpy as jnp
from jax import lax
from jax.experimental.layout import Layout, with_layout_constraint
from jax.sharding import PartitionSpec as P

QH = 32
KVH = 4
HD = 128
GROUP = 8
NEG = -1e30


def shifted(block, axis, distance):
    devices = range(lax.axis_size(axis))
    route = [(i - distance, i) for i in devices if i - distance in devices]
    return lax.ppermute(block, axis, route)


def doc_index(doc_lengths, positions):
    doc_ends = jnp.cumsum(doc_lengths)
    counted = jnp.sum((positions[:, None] >= doc_ends[None, :]).astype(jnp.int32), axis=1)
    return jnp.where(positions < 0, -1, counted)


def allowed_pairs(doc_lengths, query_pos, key_pos):
    query_docs = doc_index(doc_lengths, query_pos)
    key_docs = doc_index(doc_lengths, key_pos)
    return (query_docs[:, None] == key_docs[None, :]) & (key_pos[None, :] <= query_pos[:, None])


def scores_of(query_heads, key_heads, allowed, score_scale):
    scores = (
        jnp.einsum("tghd,sgd->ghts", query_heads, key_heads, preferred_element_type=jnp.float32)
        * score_scale
    )
    return jnp.where(allowed[None, None], scores, NEG)


def key_grad_of(grad_s, query_heads, score_scale):
    return (
        jnp.einsum("ghts,tghd->gsd", grad_s, query_heads, preferred_element_type=jnp.float32)
        * score_scale
    )


def query_grad_of(grad_s, keys):
    return jnp.einsum("ghts,sgd->ghtd", grad_s, keys, preferred_element_type=jnp.float32)


def body(queries, key_vectors, value_vectors, output_grad, doc_lengths):
    rows = queries.shape[0]
    score_scale = HD ** (-0.5)
    axes = ("ctx", "uly")
    key_value = with_layout_constraint(
        jnp.stack([key_vectors, value_vectors]), Layout(major_to_minor=(0, 1, 2))
    )
    near_rim = shifted(key_value, axes, 1)
    far_rim = shifted(key_value, axes, 2)
    device_index = lax.axis_index(axes)
    query_heads = queries.reshape(rows, KVH, GROUP, HD)
    grad_heads = output_grad.reshape(rows, KVH, GROUP, HD)
    own_keys = key_vectors.reshape(rows, KVH, HD)
    own_values = value_vectors.reshape(rows, KVH, HD)
    query_pos = device_index * rows + jnp.arange(rows, dtype=jnp.int32)
    own_pos = query_pos
    own_allowed = allowed_pairs(doc_lengths, query_pos, own_pos)
    near_allowed = allowed_pairs(doc_lengths, query_pos, own_pos - rows)
    far_allowed = allowed_pairs(doc_lengths, query_pos, own_pos - 2 * rows)

    own_scores = scores_of(query_heads, own_keys, own_allowed, score_scale)
    own_max = jnp.max(own_scores, axis=-1, keepdims=True)
    own_exp = jnp.exp(own_scores - own_max)
    own_sum = jnp.sum(own_exp, axis=-1, keepdims=True)
    own_grad_p = jnp.einsum(
        "tghd,sgd->ghts", grad_heads, own_values, preferred_element_type=jnp.float32
    )
    own_dot = jnp.sum(own_exp * own_grad_p, axis=-1, keepdims=True)

    far_keys = far_rim[0].reshape(rows, KVH, HD)
    far_values = far_rim[1].reshape(rows, KVH, HD)
    near_keys = near_rim[0].reshape(rows, KVH, HD)
    near_values = near_rim[1].reshape(rows, KVH, HD)
    far_scores = scores_of(query_heads, far_keys, far_allowed, score_scale)
    near_scores = scores_of(query_heads, near_keys, near_allowed, score_scale)
    row_max = jnp.maximum(
        own_max,
        jnp.maximum(
            jnp.max(far_scores, axis=-1, keepdims=True),
            jnp.max(near_scores, axis=-1, keepdims=True),
        ),
    )
    far_exp = jnp.exp(far_scores - row_max)
    near_exp = jnp.exp(near_scores - row_max)
    own_rescale = jnp.exp(own_max - row_max)
    row_sum = (
        own_sum * own_rescale
        + jnp.sum(far_exp, axis=-1, keepdims=True)
        + jnp.sum(near_exp, axis=-1, keepdims=True)
    )
    far_grad_p = jnp.einsum(
        "tghd,sgd->ghts", grad_heads, far_values, preferred_element_type=jnp.float32
    )
    near_grad_p = jnp.einsum(
        "tghd,sgd->ghts", grad_heads, near_values, preferred_element_type=jnp.float32
    )
    row_delta = (
        own_dot * own_rescale
        + jnp.sum(far_exp * far_grad_p, axis=-1, keepdims=True)
        + jnp.sum(near_exp * near_grad_p, axis=-1, keepdims=True)
    ) / row_sum
    far_grad_s = ((far_exp / row_sum) * (far_grad_p - row_delta)).astype(jnp.bfloat16)
    near_grad_s = ((near_exp / row_sum) * (near_grad_p - row_delta)).astype(jnp.bfloat16)
    far_key_grad = key_grad_of(far_grad_s, query_heads, score_scale)
    near_key_grad = key_grad_of(near_grad_s, query_heads, score_scale)
    far_back = shifted(far_key_grad.astype(jnp.bfloat16), axes, -2)
    near_back = shifted(near_key_grad.astype(jnp.bfloat16), axes, -1)

    own_prob = own_exp * (own_rescale / row_sum)
    own_grad_s = (own_prob * (own_grad_p - row_delta)).astype(jnp.bfloat16)
    own_key_grad = key_grad_of(own_grad_s, query_heads, score_scale)
    query_grad = (
        query_grad_of(own_grad_s, own_keys)
        + query_grad_of(far_grad_s, far_keys)
        + query_grad_of(near_grad_s, near_keys)
    ) * score_scale
    query_grad = jnp.transpose(query_grad.astype(jnp.bfloat16), (2, 0, 1, 3)).reshape(rows, QH * HD)
    key_grad = own_key_grad + near_back.astype(jnp.float32) + far_back.astype(jnp.float32)
    key_grad = jnp.transpose(key_grad, (1, 0, 2)).reshape(rows, KVH * HD).astype(jnp.bfloat16)
    return (query_grad, key_grad)


def solution(mesh):
    placed = (
        P(("dp", "ctx", "uly"), None),
        P(("dp", "ctx", "uly"), None),
        P(("dp", "ctx", "uly"), None),
        P(("dp", "ctx", "uly"), None),
        P("dp"),
    )
    return jax.shard_map(
        body,
        mesh=mesh,
        in_specs=placed,
        out_specs=(P(("dp", "ctx", "uly"), None), P(("dp", "ctx", "uly"), None)),
        check_vma=False,
    )
```

```python
import jax
import jax.numpy as jnp
from jax import lax
from jax.sharding import PartitionSpec as P

QH = 32
KVH = 4
HD = 128
GROUP = 8
NEG = -1e30


def shifted(block, axis, distance):
    devices = range(lax.axis_size(axis))
    route = [(i - distance, i) for i in devices if i - distance in devices]
    return lax.ppermute(block, axis, route)


def doc_index(doc_lengths, positions):
    doc_ends = jnp.cumsum(doc_lengths)
    counted = jnp.sum((positions[:, None] >= doc_ends[None, :]).astype(jnp.int32), axis=1)
    return jnp.where(positions < 0, -1, counted)


def allowed_pairs(doc_lengths, query_pos, key_pos):
    query_docs = doc_index(doc_lengths, query_pos)
    key_docs = doc_index(doc_lengths, key_pos)
    return (query_docs[:, None] == key_docs[None, :]) & (key_pos[None, :] <= query_pos[:, None])


def scores_of(query_heads, key_heads, allowed, score_scale):
    scores = (
        jnp.einsum("tghd,sgd->ghts", query_heads, key_heads, preferred_element_type=jnp.float32)
        * score_scale
    )
    return jnp.where(allowed[None, None], scores, NEG)


def key_grad_of(grad_s, query_heads, score_scale):
    return (
        jnp.einsum("ghts,tghd->gsd", grad_s, query_heads, preferred_element_type=jnp.float32)
        * score_scale
    )


def query_grad_of(grad_s, keys):
    return jnp.einsum("ghts,sgd->ghtd", grad_s, keys, preferred_element_type=jnp.float32)


def body(queries, key_vectors, value_vectors, output_grad, doc_lengths):
    rows = queries.shape[0]
    score_scale = HD ** (-0.5)
    axes = ("ctx", "uly")
    key_value = jnp.stack([key_vectors, value_vectors])
    near_rim = shifted(key_value, axes, 1)
    far_rim = shifted(key_value, axes, 2)
    device_index = lax.axis_index(axes)
    query_heads = queries.reshape(rows, KVH, GROUP, HD)
    grad_heads = output_grad.reshape(rows, KVH, GROUP, HD)
    own_keys = key_vectors.reshape(rows, KVH, HD)
    own_values = value_vectors.reshape(rows, KVH, HD)
    query_pos = device_index * rows + jnp.arange(rows, dtype=jnp.int32)
    own_pos = query_pos
    own_allowed = allowed_pairs(doc_lengths, query_pos, own_pos)
    near_allowed = allowed_pairs(doc_lengths, query_pos, own_pos - rows)
    far_allowed = allowed_pairs(doc_lengths, query_pos, own_pos - 2 * rows)

    own_scores = scores_of(query_heads, own_keys, own_allowed, score_scale)
    own_max = jnp.max(own_scores, axis=-1, keepdims=True)
    own_exp = jnp.exp(own_scores - own_max)
    own_sum = jnp.sum(own_exp, axis=-1, keepdims=True)
    own_grad_p = jnp.einsum(
        "tghd,sgd->ghts", grad_heads, own_values, preferred_element_type=jnp.float32
    )
    own_dot = jnp.sum(own_exp * own_grad_p, axis=-1, keepdims=True)

    far_keys = far_rim[0].reshape(rows, KVH, HD)
    far_values = far_rim[1].reshape(rows, KVH, HD)
    near_keys = near_rim[0].reshape(rows, KVH, HD)
    near_values = near_rim[1].reshape(rows, KVH, HD)
    far_scores = scores_of(query_heads, far_keys, far_allowed, score_scale)
    near_scores = scores_of(query_heads, near_keys, near_allowed, score_scale)
    row_max = jnp.maximum(
        own_max,
        jnp.maximum(
            jnp.max(far_scores, axis=-1, keepdims=True),
            jnp.max(near_scores, axis=-1, keepdims=True),
        ),
    )
    far_exp = jnp.exp(far_scores - row_max)
    near_exp = jnp.exp(near_scores - row_max)
    own_rescale = jnp.exp(own_max - row_max)
    row_sum = (
        own_sum * own_rescale
        + jnp.sum(far_exp, axis=-1, keepdims=True)
        + jnp.sum(near_exp, axis=-1, keepdims=True)
    )
    far_grad_p = jnp.einsum(
        "tghd,sgd->ghts", grad_heads, far_values, preferred_element_type=jnp.float32
    )
    near_grad_p = jnp.einsum(
        "tghd,sgd->ghts", grad_heads, near_values, preferred_element_type=jnp.float32
    )
    row_delta = (
        own_dot * own_rescale
        + jnp.sum(far_exp * far_grad_p, axis=-1, keepdims=True)
        + jnp.sum(near_exp * near_grad_p, axis=-1, keepdims=True)
    ) / row_sum
    far_grad_s = ((far_exp / row_sum) * (far_grad_p - row_delta)).astype(jnp.bfloat16)
    near_grad_s = ((near_exp / row_sum) * (near_grad_p - row_delta)).astype(jnp.bfloat16)
    far_key_grad = key_grad_of(far_grad_s, query_heads, score_scale)
    near_key_grad = key_grad_of(near_grad_s, query_heads, score_scale)
    far_key_grad = far_key_grad.astype(jnp.bfloat16)
    near_key_grad = near_key_grad.astype(jnp.bfloat16)
    far_back = shifted(far_key_grad, axes, -2)
    near_back = shifted(near_key_grad, axes, -1)

    _, own_scale, row_delta, far_grad_s, near_grad_s = lax.optimization_barrier(
        ((far_key_grad, near_key_grad), own_rescale / row_sum, row_delta, far_grad_s, near_grad_s)
    )
    own_prob = own_exp * own_scale
    own_grad_s = (own_prob * (own_grad_p - row_delta)).astype(jnp.bfloat16)
    own_key_grad = key_grad_of(own_grad_s, query_heads, score_scale)
    query_grad = (
        query_grad_of(own_grad_s, own_keys)
        + query_grad_of(far_grad_s, far_keys)
        + query_grad_of(near_grad_s, near_keys)
    ) * score_scale
    query_grad = jnp.transpose(query_grad.astype(jnp.bfloat16), (2, 0, 1, 3)).reshape(rows, QH * HD)
    key_grad = own_key_grad + near_back.astype(jnp.float32) + far_back.astype(jnp.float32)
    key_grad = jnp.transpose(key_grad, (1, 0, 2)).reshape(rows, KVH * HD).astype(jnp.bfloat16)
    return (query_grad, key_grad)


def solution(mesh):
    placed = (
        P(("dp", "ctx", "uly"), None),
        P(("dp", "ctx", "uly"), None),
        P(("dp", "ctx", "uly"), None),
        P(("dp", "ctx", "uly"), None),
        P("dp"),
    )
    return jax.shard_map(
        body,
        mesh=mesh,
        in_specs=placed,
        out_specs=(P(("dp", "ctx", "uly"), None), P(("dp", "ctx", "uly"), None)),
        check_vma=False,
    )
```

```python
import jax
import jax.numpy as jnp
from jax import lax
from jax.sharding import PartitionSpec as P

QH = 32
KVH = 4
HD = 128
GROUP = 8
NEG = -1e30


def shifted(block, axis, distance):
    devices = range(lax.axis_size(axis))
    route = [(i - distance, i) for i in devices if i - distance in devices]
    return lax.ppermute(block, axis, route)


def doc_index(doc_lengths, positions):
    doc_ends = jnp.cumsum(doc_lengths)
    counted = jnp.sum((positions[:, None] >= doc_ends[None, :]).astype(jnp.int32), axis=1)
    return jnp.where(positions < 0, -1, counted)


def allowed_pairs(doc_lengths, query_pos, key_pos):
    query_docs = doc_index(doc_lengths, query_pos)
    key_docs = doc_index(doc_lengths, key_pos)
    return (query_docs[:, None] == key_docs[None, :]) & (key_pos[None, :] <= query_pos[:, None])


def scores_of(query_heads, key_heads, allowed, score_scale):
    scores = (
        jnp.einsum("tghd,sgd->ghts", query_heads, key_heads, preferred_element_type=jnp.float32)
        * score_scale
    )
    return jnp.where(allowed[None, None], scores, NEG)


def key_grad_of(grad_s, query_heads, score_scale):
    return (
        jnp.einsum("ghts,tghd->gsd", grad_s, query_heads, preferred_element_type=jnp.float32)
        * score_scale
    )


def query_grad_of(grad_s, keys):
    return jnp.einsum("ghts,sgd->ghtd", grad_s, keys, preferred_element_type=jnp.float32)


def body(queries, key_vectors, value_vectors, output_grad, doc_lengths):
    rows = queries.shape[0]
    score_scale = HD ** (-0.5)
    axes = ("ctx", "uly")
    key_value = jnp.stack([key_vectors, value_vectors])
    near_rim = shifted(key_value, axes, 1)
    far_rim = shifted(key_value, axes, 2)
    device_index = lax.axis_index(axes)
    query_heads = queries.reshape(rows, KVH, GROUP, HD)
    grad_heads = output_grad.reshape(rows, KVH, GROUP, HD)
    own_keys = key_vectors.reshape(rows, KVH, HD)
    own_values = value_vectors.reshape(rows, KVH, HD)
    query_pos = device_index * rows + jnp.arange(rows, dtype=jnp.int32)
    own_pos = query_pos
    own_allowed = allowed_pairs(doc_lengths, query_pos, own_pos)
    near_allowed = allowed_pairs(doc_lengths, query_pos, own_pos - rows)
    far_allowed = allowed_pairs(doc_lengths, query_pos, own_pos - 2 * rows)

    own_scores = scores_of(query_heads, own_keys, own_allowed, score_scale)
    own_max = jnp.max(own_scores, axis=-1, keepdims=True)
    own_exp = jnp.exp(own_scores - own_max)
    own_sum = jnp.sum(own_exp, axis=-1, keepdims=True)
    own_grad_p = jnp.einsum(
        "tghd,sgd->ghts", grad_heads, own_values, preferred_element_type=jnp.float32
    )
    own_dot = jnp.sum(own_exp * own_grad_p, axis=-1, keepdims=True)

    far_keys = far_rim[0].reshape(rows, KVH, HD)
    far_values = far_rim[1].reshape(rows, KVH, HD)
    near_keys = near_rim[0].reshape(rows, KVH, HD)
    near_values = near_rim[1].reshape(rows, KVH, HD)
    far_scores = scores_of(query_heads, far_keys, far_allowed, score_scale)
    near_scores = scores_of(query_heads, near_keys, near_allowed, score_scale)
    row_max = jnp.maximum(
        own_max,
        jnp.maximum(
            jnp.max(far_scores, axis=-1, keepdims=True),
            jnp.max(near_scores, axis=-1, keepdims=True),
        ),
    )
    far_exp = jnp.exp(far_scores - row_max)
    near_exp = jnp.exp(near_scores - row_max)
    own_rescale = jnp.exp(own_max - row_max)
    row_sum = (
        own_sum * own_rescale
        + jnp.sum(far_exp, axis=-1, keepdims=True)
        + jnp.sum(near_exp, axis=-1, keepdims=True)
    )
    far_grad_p = jnp.einsum(
        "tghd,sgd->ghts", grad_heads, far_values, preferred_element_type=jnp.float32
    )
    near_grad_p = jnp.einsum(
        "tghd,sgd->ghts", grad_heads, near_values, preferred_element_type=jnp.float32
    )
    row_delta = (
        own_dot * own_rescale
        + jnp.sum(far_exp * far_grad_p, axis=-1, keepdims=True)
        + jnp.sum(near_exp * near_grad_p, axis=-1, keepdims=True)
    ) / row_sum
    far_grad_s = ((far_exp / row_sum) * (far_grad_p - row_delta)).astype(jnp.bfloat16)
    near_grad_s = ((near_exp / row_sum) * (near_grad_p - row_delta)).astype(jnp.bfloat16)
    far_key_grad = key_grad_of(far_grad_s, query_heads, score_scale)
    near_key_grad = key_grad_of(near_grad_s, query_heads, score_scale)
    far_key_grad = far_key_grad.astype(jnp.bfloat16)
    near_key_grad = near_key_grad.astype(jnp.bfloat16)
    far_back = shifted(far_key_grad, axes, -2)
    near_back = shifted(near_key_grad, axes, -1)

    _, own_scale, row_delta, far_grad_s, near_grad_s = lax.optimization_barrier(
        ((far_key_grad, near_key_grad), own_rescale / row_sum, row_delta, far_grad_s, near_grad_s)
    )
    own_prob = own_exp * own_scale
    own_grad_s = (own_prob * (own_grad_p - row_delta)).astype(jnp.bfloat16)
    own_key_grad = key_grad_of(own_grad_s, query_heads, score_scale)
    query_grad = (
        query_grad_of(own_grad_s, own_keys)
        + query_grad_of(far_grad_s, far_keys)
        + query_grad_of(near_grad_s, near_keys)
    ) * score_scale
    query_grad = jnp.transpose(query_grad.astype(jnp.bfloat16), (2, 0, 1, 3)).reshape(rows, QH * HD)
    key_grad = own_key_grad + near_back.astype(jnp.float32) + far_back.astype(jnp.float32)
    key_grad = jnp.concatenate([key_grad[g] for g in range(KVH)], axis=1).astype(jnp.bfloat16)
    return (query_grad, key_grad)


def solution(mesh):
    placed = (
        P(("dp", "ctx", "uly"), None),
        P(("dp", "ctx", "uly"), None),
        P(("dp", "ctx", "uly"), None),
        P(("dp", "ctx", "uly"), None),
        P("dp"),
    )
    return jax.shard_map(
        body,
        mesh=mesh,
        in_specs=placed,
        out_specs=(P(("dp", "ctx", "uly"), None), P(("dp", "ctx", "uly"), None)),
        check_vma=False,
    )
```

```python
import jax
import jax.numpy as jnp
from jax import lax
from jax.sharding import PartitionSpec as P

QH = 32
KVH = 4
HD = 128
GROUP = 8
NEG = -1e30


def shifted(block, axis, distance):
    devices = range(lax.axis_size(axis))
    route = [(i - distance, i) for i in devices if i - distance in devices]
    return lax.ppermute(block, axis, route)


def doc_index(doc_lengths, positions):
    doc_ends = jnp.cumsum(doc_lengths)
    counted = jnp.sum((positions[:, None] >= doc_ends[None, :]).astype(jnp.int32), axis=1)
    return jnp.where(positions < 0, -1, counted)


def allowed_pairs(doc_lengths, query_pos, key_pos):
    query_docs = doc_index(doc_lengths, query_pos)
    key_docs = doc_index(doc_lengths, key_pos)
    return (query_docs[:, None] == key_docs[None, :]) & (key_pos[None, :] <= query_pos[:, None])


def scores_of(query_heads, key_heads, allowed, score_scale):
    scores = (
        jnp.einsum("tghd,sgd->ghts", query_heads, key_heads, preferred_element_type=jnp.float32)
        * score_scale
    )
    return jnp.where(allowed[None, None], scores, NEG)


def key_grad_of(grad_s, query_heads, score_scale):
    return (
        jnp.einsum("ghts,tghd->gsd", grad_s, query_heads, preferred_element_type=jnp.float32)
        * score_scale
    )


def query_grad_of(grad_s, keys):
    return jnp.einsum("ghts,sgd->ghtd", grad_s, keys, preferred_element_type=jnp.float32)


def body(queries, key_vectors, value_vectors, output_grad, doc_lengths):
    rows = queries.shape[0]
    score_scale = HD ** (-0.5)
    axes = ("ctx", "uly")
    key_value = jnp.stack([key_vectors, value_vectors])
    far_rim = shifted(key_value, axes, 2)
    near_rim = shifted(key_value, axes, 1)
    device_index = lax.axis_index(axes)
    query_heads = queries.reshape(rows, KVH, GROUP, HD)
    grad_heads = output_grad.reshape(rows, KVH, GROUP, HD)
    own_keys = key_vectors.reshape(rows, KVH, HD)
    own_values = value_vectors.reshape(rows, KVH, HD)
    query_pos = device_index * rows + jnp.arange(rows, dtype=jnp.int32)
    own_pos = query_pos
    own_allowed = allowed_pairs(doc_lengths, query_pos, own_pos)
    near_allowed = allowed_pairs(doc_lengths, query_pos, own_pos - rows)
    far_allowed = allowed_pairs(doc_lengths, query_pos, own_pos - 2 * rows)

    own_scores = scores_of(query_heads, own_keys, own_allowed, score_scale)
    own_max = jnp.max(own_scores, axis=-1, keepdims=True)
    own_exp = jnp.exp(own_scores - own_max)
    own_sum = jnp.sum(own_exp, axis=-1, keepdims=True)
    own_grad_p = jnp.einsum(
        "tghd,sgd->ghts", grad_heads, own_values, preferred_element_type=jnp.float32
    )
    own_dot = jnp.sum(own_exp * own_grad_p, axis=-1, keepdims=True)

    near_keys = near_rim[0].reshape(rows, KVH, HD)
    near_values = near_rim[1].reshape(rows, KVH, HD)
    near_scores = scores_of(query_heads, near_keys, near_allowed, score_scale)
    near_max = jnp.max(near_scores, axis=-1, keepdims=True)
    near_exp = jnp.exp(near_scores - near_max)
    near_sum = jnp.sum(near_exp, axis=-1, keepdims=True)
    near_grad_p = jnp.einsum(
        "tghd,sgd->ghts", grad_heads, near_values, preferred_element_type=jnp.float32
    )
    near_dot = jnp.sum(near_exp * near_grad_p, axis=-1, keepdims=True)
    near_stats, far_rim = lax.optimization_barrier(
        ((near_max, near_exp, near_sum, near_grad_p, near_dot), far_rim)
    )
    near_max, near_exp, near_sum, near_grad_p, near_dot = near_stats

    far_keys = far_rim[0].reshape(rows, KVH, HD)
    far_values = far_rim[1].reshape(rows, KVH, HD)
    far_scores = scores_of(query_heads, far_keys, far_allowed, score_scale)
    row_max = jnp.maximum(
        jnp.maximum(own_max, near_max), jnp.max(far_scores, axis=-1, keepdims=True)
    )
    far_exp = jnp.exp(far_scores - row_max)
    own_rescale = jnp.exp(own_max - row_max)
    near_rescale = jnp.exp(near_max - row_max)
    row_sum = (
        own_sum * own_rescale
        + near_sum * near_rescale
        + jnp.sum(far_exp, axis=-1, keepdims=True)
    )
    far_grad_p = jnp.einsum(
        "tghd,sgd->ghts", grad_heads, far_values, preferred_element_type=jnp.float32
    )
    row_delta = (
        own_dot * own_rescale
        + near_dot * near_rescale
        + jnp.sum(far_exp * far_grad_p, axis=-1, keepdims=True)
    ) / row_sum
    near_exp = near_exp * near_rescale
    far_grad_s = ((far_exp / row_sum) * (far_grad_p - row_delta)).astype(jnp.bfloat16)
    near_grad_s = ((near_exp / row_sum) * (near_grad_p - row_delta)).astype(jnp.bfloat16)
    far_key_grad = key_grad_of(far_grad_s, query_heads, score_scale)
    near_key_grad = key_grad_of(near_grad_s, query_heads, score_scale)
    far_key_grad = far_key_grad.astype(jnp.bfloat16)
    near_key_grad = near_key_grad.astype(jnp.bfloat16)
    far_back = shifted(far_key_grad, axes, -2)
    near_back = shifted(near_key_grad, axes, -1)

    _, own_scale, row_delta, far_grad_s, near_grad_s = lax.optimization_barrier(
        ((far_key_grad, near_key_grad), own_rescale / row_sum, row_delta, far_grad_s, near_grad_s)
    )
    own_prob = own_exp * own_scale
    own_grad_s = (own_prob * (own_grad_p - row_delta)).astype(jnp.bfloat16)
    own_key_grad = key_grad_of(own_grad_s, query_heads, score_scale)
    query_grad = (
        query_grad_of(own_grad_s, own_keys)
        + query_grad_of(far_grad_s, far_keys)
        + query_grad_of(near_grad_s, near_keys)
    ) * score_scale
    query_grad = jnp.transpose(query_grad.astype(jnp.bfloat16), (2, 0, 1, 3)).reshape(rows, QH * HD)
    key_grad = own_key_grad + near_back.astype(jnp.float32) + far_back.astype(jnp.float32)
    key_grad = jnp.concatenate([key_grad[g] for g in range(KVH)], axis=1).astype(jnp.bfloat16)
    return (query_grad, key_grad)


def solution(mesh):
    placed = (
        P(("dp", "ctx", "uly"), None),
        P(("dp", "ctx", "uly"), None),
        P(("dp", "ctx", "uly"), None),
        P(("dp", "ctx", "uly"), None),
        P("dp"),
    )
    return jax.shard_map(
        body,
        mesh=mesh,
        in_specs=placed,
        out_specs=(P(("dp", "ctx", "uly"), None), P(("dp", "ctx", "uly"), None)),
        check_vma=False,
    )
```

```python
import jax
import jax.numpy as jnp
from jax import lax
from jax.sharding import PartitionSpec as P

QH = 32
KVH = 4
HD = 128
GROUP = 8
NEG = -1e30


def shifted(block, axis, distance):
    devices = range(lax.axis_size(axis))
    route = [(i - distance, i) for i in devices if i - distance in devices]
    return lax.ppermute(block, axis, route)


def doc_index(doc_lengths, positions):
    doc_ends = jnp.cumsum(doc_lengths)
    counted = jnp.sum((positions[:, None] >= doc_ends[None, :]).astype(jnp.int32), axis=1)
    return jnp.where(positions < 0, -1, counted)


def allowed_pairs(doc_lengths, query_pos, key_pos):
    query_docs = doc_index(doc_lengths, query_pos)
    key_docs = doc_index(doc_lengths, key_pos)
    return (query_docs[:, None] == key_docs[None, :]) & (key_pos[None, :] <= query_pos[:, None])


def scores_of(query_heads, key_heads, allowed, score_scale):
    scores = (
        jnp.einsum("tghd,sgd->ghts", query_heads, key_heads, preferred_element_type=jnp.float32)
        * score_scale
    )
    return jnp.where(allowed[None, None], scores, NEG)


def key_grad_of(grad_s, query_heads, score_scale):
    return (
        jnp.einsum("ghts,tghd->gsd", grad_s, query_heads, preferred_element_type=jnp.float32)
        * score_scale
    )


def query_grad_of(grad_s, keys):
    return jnp.einsum("ghts,sgd->ghtd", grad_s, keys, preferred_element_type=jnp.float32)


def body(queries, key_vectors, value_vectors, output_grad, doc_lengths):
    rows = queries.shape[0]
    score_scale = HD ** (-0.5)
    axes = ("ctx", "uly")
    key_value = jnp.stack([key_vectors, value_vectors])
    near_rim = shifted(key_value, axes, 1)
    far_rim = shifted(key_value, axes, 2)
    device_index = lax.axis_index(axes)
    query_heads = queries.reshape(rows, KVH, GROUP, HD)
    grad_heads = output_grad.reshape(rows, KVH, GROUP, HD)
    own_keys = key_vectors.reshape(rows, KVH, HD)
    own_values = value_vectors.reshape(rows, KVH, HD)
    query_pos = device_index * rows + jnp.arange(rows, dtype=jnp.int32)
    own_pos = query_pos
    own_allowed = allowed_pairs(doc_lengths, query_pos, own_pos)
    near_allowed = allowed_pairs(doc_lengths, query_pos, own_pos - rows)
    far_allowed = allowed_pairs(doc_lengths, query_pos, own_pos - 2 * rows)

    own_scores = scores_of(query_heads, own_keys, own_allowed, score_scale)
    own_max = jnp.max(own_scores, axis=-1, keepdims=True)
    own_exp = jnp.exp(own_scores - own_max)
    own_sum = jnp.sum(own_exp, axis=-1, keepdims=True)
    own_grad_p = jnp.einsum(
        "tghd,sgd->ghts", grad_heads, own_values, preferred_element_type=jnp.float32
    )
    own_dot = jnp.sum(own_exp * own_grad_p, axis=-1, keepdims=True)

    far_keys = far_rim[0].reshape(rows, KVH, HD)
    far_values = far_rim[1].reshape(rows, KVH, HD)
    near_keys = near_rim[0].reshape(rows, KVH, HD)
    near_values = near_rim[1].reshape(rows, KVH, HD)
    far_scores = scores_of(query_heads, far_keys, far_allowed, score_scale)
    near_scores = scores_of(query_heads, near_keys, near_allowed, score_scale)
    row_max = jnp.maximum(
        own_max,
        jnp.maximum(
            jnp.max(far_scores, axis=-1, keepdims=True),
            jnp.max(near_scores, axis=-1, keepdims=True),
        ),
    )
    far_exp = jnp.exp(far_scores - row_max)
    near_exp = jnp.exp(near_scores - row_max)
    own_rescale = jnp.exp(own_max - row_max)
    row_sum = (
        own_sum * own_rescale
        + jnp.sum(far_exp, axis=-1, keepdims=True)
        + jnp.sum(near_exp, axis=-1, keepdims=True)
    )
    far_grad_p = jnp.einsum(
        "tghd,sgd->ghts", grad_heads, far_values, preferred_element_type=jnp.float32
    )
    near_grad_p = jnp.einsum(
        "tghd,sgd->ghts", grad_heads, near_values, preferred_element_type=jnp.float32
    )
    row_delta = (
        own_dot * own_rescale
        + jnp.sum(far_exp * far_grad_p, axis=-1, keepdims=True)
        + jnp.sum(near_exp * near_grad_p, axis=-1, keepdims=True)
    ) / row_sum
    far_grad_s = ((far_exp / row_sum) * (far_grad_p - row_delta)).astype(jnp.bfloat16)
    near_grad_s = ((near_exp / row_sum) * (near_grad_p - row_delta)).astype(jnp.bfloat16)
    far_key_grad = key_grad_of(far_grad_s, query_heads, score_scale).astype(jnp.bfloat16)
    far_back = shifted(far_key_grad, axes, -2)
    far_key_grad, near_grad_s = lax.optimization_barrier((far_key_grad, near_grad_s))
    near_key_grad = key_grad_of(near_grad_s, query_heads, score_scale).astype(jnp.bfloat16)
    near_back = shifted(near_key_grad, axes, -1)

    _, own_scale, row_delta, far_grad_s, near_grad_s = lax.optimization_barrier(
        ((far_key_grad, near_key_grad), own_rescale / row_sum, row_delta, far_grad_s, near_grad_s)
    )
    own_prob = own_exp * own_scale
    own_grad_s = (own_prob * (own_grad_p - row_delta)).astype(jnp.bfloat16)
    own_key_grad = key_grad_of(own_grad_s, query_heads, score_scale)
    query_grad = (
        query_grad_of(own_grad_s, own_keys)
        + query_grad_of(far_grad_s, far_keys)
        + query_grad_of(near_grad_s, near_keys)
    ) * score_scale
    query_grad = jnp.transpose(query_grad.astype(jnp.bfloat16), (2, 0, 1, 3)).reshape(rows, QH * HD)
    key_grad = own_key_grad + near_back.astype(jnp.float32) + far_back.astype(jnp.float32)
    key_grad = jnp.concatenate([key_grad[g] for g in range(KVH)], axis=1).astype(jnp.bfloat16)
    return (query_grad, key_grad)


def solution(mesh):
    placed = (
        P(("dp", "ctx", "uly"), None),
        P(("dp", "ctx", "uly"), None),
        P(("dp", "ctx", "uly"), None),
        P(("dp", "ctx", "uly"), None),
        P("dp"),
    )
    return jax.shard_map(
        body,
        mesh=mesh,
        in_specs=placed,
        out_specs=(P(("dp", "ctx", "uly"), None), P(("dp", "ctx", "uly"), None)),
        check_vma=False,
    )
```

```python
import jax
import jax.numpy as jnp
from jax import lax
from jax.sharding import PartitionSpec as P

QH = 32
KVH = 4
HD = 128
GROUP = 8
NEG = -1e30


def shifted(block, axis, distance):
    devices = range(lax.axis_size(axis))
    route = [(i - distance, i) for i in devices if i - distance in devices]
    return lax.ppermute(block, axis, route)


def doc_index(doc_lengths, positions):
    doc_ends = jnp.cumsum(doc_lengths)
    counted = jnp.sum((positions[:, None] >= doc_ends[None, :]).astype(jnp.int32), axis=1)
    return jnp.where(positions < 0, -1, counted)


def allowed_pairs(doc_lengths, query_pos, key_pos):
    query_docs = doc_index(doc_lengths, query_pos)
    key_docs = doc_index(doc_lengths, key_pos)
    return (query_docs[:, None] == key_docs[None, :]) & (key_pos[None, :] <= query_pos[:, None])


def scores_of(query_heads, key_heads, allowed, score_scale):
    scores = (
        jnp.einsum("tghd,sgd->ghts", query_heads, key_heads, preferred_element_type=jnp.float32)
        * score_scale
    )
    return jnp.where(allowed[None, None], scores, NEG)


def key_grad_of(grad_s, query_heads, score_scale):
    return (
        jnp.einsum("ghts,tghd->gsd", grad_s, query_heads, preferred_element_type=jnp.float32)
        * score_scale
    )


def query_grad_of(grad_s, keys):
    return jnp.einsum("ghts,sgd->ghtd", grad_s, keys, preferred_element_type=jnp.float32)


def body(queries, key_vectors, value_vectors, output_grad, doc_lengths):
    rows = queries.shape[0]
    score_scale = HD ** (-0.5)
    axes = ("ctx", "uly")
    key_value = jnp.stack([key_vectors, value_vectors])
    near_rim = shifted(key_value, axes, 1)
    far_rim = shifted(key_value, axes, 2)
    device_index = lax.axis_index(axes)
    query_heads = queries.reshape(rows, KVH, GROUP, HD)
    grad_heads = output_grad.reshape(rows, KVH, GROUP, HD)
    own_keys = key_vectors.reshape(rows, KVH, HD)
    own_values = value_vectors.reshape(rows, KVH, HD)
    query_pos = device_index * rows + jnp.arange(rows, dtype=jnp.int32)
    own_pos = query_pos
    own_allowed = allowed_pairs(doc_lengths, query_pos, own_pos)
    near_allowed = allowed_pairs(doc_lengths, query_pos, own_pos - rows)
    far_allowed = allowed_pairs(doc_lengths, query_pos, own_pos - 2 * rows)

    own_scores = scores_of(query_heads, own_keys, own_allowed, score_scale)
    own_max = jnp.max(own_scores, axis=-1, keepdims=True)
    own_exp = jnp.exp(own_scores - own_max)
    own_sum = jnp.sum(own_exp, axis=-1, keepdims=True)
    own_grad_p = jnp.einsum(
        "tghd,sgd->ghts", grad_heads, own_values, preferred_element_type=jnp.float32
    )
    own_dot = jnp.sum(own_exp * own_grad_p, axis=-1, keepdims=True)

    far_keys = far_rim[0].reshape(rows, KVH, HD)
    far_values = far_rim[1].reshape(rows, KVH, HD)
    near_keys = near_rim[0].reshape(rows, KVH, HD)
    near_values = near_rim[1].reshape(rows, KVH, HD)
    far_scores = scores_of(query_heads, far_keys, far_allowed, score_scale)
    near_scores = scores_of(query_heads, near_keys, near_allowed, score_scale)
    row_max = jnp.maximum(
        own_max,
        jnp.maximum(
            jnp.max(far_scores, axis=-1, keepdims=True),
            jnp.max(near_scores, axis=-1, keepdims=True),
        ),
    )
    far_exp = jnp.exp(far_scores - row_max)
    near_exp = jnp.exp(near_scores - row_max)
    own_rescale = jnp.exp(own_max - row_max)
    row_sum = (
        own_sum * own_rescale
        + jnp.sum(far_exp, axis=-1, keepdims=True)
        + jnp.sum(near_exp, axis=-1, keepdims=True)
    )
    far_grad_p = jnp.einsum(
        "tghd,sgd->ghts", grad_heads, far_values, preferred_element_type=jnp.float32
    )
    near_grad_p = jnp.einsum(
        "tghd,sgd->ghts", grad_heads, near_values, preferred_element_type=jnp.float32
    )
    row_delta = (
        own_dot * own_rescale
        + jnp.sum(far_exp * far_grad_p, axis=-1, keepdims=True)
        + jnp.sum(near_exp * near_grad_p, axis=-1, keepdims=True)
    ) / row_sum
    far_grad_s = ((far_exp / row_sum) * (far_grad_p - row_delta)).astype(jnp.bfloat16)
    far_key_grad = key_grad_of(far_grad_s, query_heads, score_scale).astype(jnp.bfloat16)
    far_back = shifted(far_key_grad, axes, -2)
    far_key_grad, near_exp, near_grad_p, near_delta, near_sum = lax.optimization_barrier(
        (far_key_grad, near_exp, near_grad_p, row_delta, row_sum)
    )
    near_grad_s = ((near_exp / near_sum) * (near_grad_p - near_delta)).astype(jnp.bfloat16)
    near_key_grad = key_grad_of(near_grad_s, query_heads, score_scale).astype(jnp.bfloat16)
    near_back = shifted(near_key_grad, axes, -1)

    _, own_scale, row_delta, far_grad_s, near_grad_s = lax.optimization_barrier(
        ((far_key_grad, near_key_grad), own_rescale / row_sum, row_delta, far_grad_s, near_grad_s)
    )
    own_prob = own_exp * own_scale
    own_grad_s = (own_prob * (own_grad_p - row_delta)).astype(jnp.bfloat16)
    own_key_grad = key_grad_of(own_grad_s, query_heads, score_scale)
    query_grad = (
        query_grad_of(own_grad_s, own_keys)
        + query_grad_of(far_grad_s, far_keys)
        + query_grad_of(near_grad_s, near_keys)
    ) * score_scale
    query_grad = jnp.transpose(query_grad.astype(jnp.bfloat16), (2, 0, 1, 3)).reshape(rows, QH * HD)
    key_grad = own_key_grad + near_back.astype(jnp.float32) + far_back.astype(jnp.float32)
    key_grad = jnp.concatenate([key_grad[g] for g in range(KVH)], axis=1).astype(jnp.bfloat16)
    return (query_grad, key_grad)


def solution(mesh):
    placed = (
        P(("dp", "ctx", "uly"), None),
        P(("dp", "ctx", "uly"), None),
        P(("dp", "ctx", "uly"), None),
        P(("dp", "ctx", "uly"), None),
        P("dp"),
    )
    return jax.shard_map(
        body,
        mesh=mesh,
        in_specs=placed,
        out_specs=(P(("dp", "ctx", "uly"), None), P(("dp", "ctx", "uly"), None)),
        check_vma=False,
    )
```

```python
import jax
import jax.numpy as jnp
from jax import lax
from jax.sharding import PartitionSpec as P

QH = 32
KVH = 4
HD = 128
GROUP = 8
NEG = -1e30


def shifted(block, axis, distance):
    devices = range(lax.axis_size(axis))
    route = [(i - distance, i) for i in devices if i - distance in devices]
    return lax.ppermute(block, axis, route)


def doc_index(doc_lengths, positions):
    doc_ends = jnp.cumsum(doc_lengths)
    counted = jnp.sum((positions[:, None] >= doc_ends[None, :]).astype(jnp.int32), axis=1)
    return jnp.where(positions < 0, -1, counted)


def allowed_pairs(doc_lengths, query_pos, key_pos):
    query_docs = doc_index(doc_lengths, query_pos)
    key_docs = doc_index(doc_lengths, key_pos)
    return (query_docs[:, None] == key_docs[None, :]) & (key_pos[None, :] <= query_pos[:, None])


def scores_of(query_heads, key_heads, allowed, score_scale):
    scores = (
        jnp.einsum("tghd,sgd->ghts", query_heads, key_heads, preferred_element_type=jnp.float32)
        * score_scale
    )
    return jnp.where(allowed[None, None], scores, NEG)


def key_grad_of(grad_s, query_heads, score_scale):
    return (
        jnp.einsum("ghts,tghd->gsd", grad_s, query_heads, preferred_element_type=jnp.float32)
        * score_scale
    )


def query_grad_of(grad_s, keys):
    return jnp.einsum("ghts,sgd->ghtd", grad_s, keys, preferred_element_type=jnp.float32)


def body(queries, key_vectors, value_vectors, output_grad, doc_lengths):
    rows = queries.shape[0]
    score_scale = HD ** (-0.5)
    axes = ("ctx", "uly")
    key_value = jnp.stack([key_vectors, value_vectors])
    near_rim = shifted(key_value, axes, 1)
    far_rim = (shifted(key_vectors, axes, 2), shifted(value_vectors, axes, 2))
    device_index = lax.axis_index(axes)
    query_heads = queries.reshape(rows, KVH, GROUP, HD)
    grad_heads = output_grad.reshape(rows, KVH, GROUP, HD)
    own_keys = key_vectors.reshape(rows, KVH, HD)
    own_values = value_vectors.reshape(rows, KVH, HD)
    query_pos = device_index * rows + jnp.arange(rows, dtype=jnp.int32)
    own_pos = query_pos
    own_allowed = allowed_pairs(doc_lengths, query_pos, own_pos)
    near_allowed = allowed_pairs(doc_lengths, query_pos, own_pos - rows)
    far_allowed = allowed_pairs(doc_lengths, query_pos, own_pos - 2 * rows)

    own_scores = scores_of(query_heads, own_keys, own_allowed, score_scale)
    own_max = jnp.max(own_scores, axis=-1, keepdims=True)
    own_exp = jnp.exp(own_scores - own_max)
    own_sum = jnp.sum(own_exp, axis=-1, keepdims=True)
    own_grad_p = jnp.einsum(
        "tghd,sgd->ghts", grad_heads, own_values, preferred_element_type=jnp.float32
    )
    own_dot = jnp.sum(own_exp * own_grad_p, axis=-1, keepdims=True)

    far_keys = far_rim[0].reshape(rows, KVH, HD)
    far_values = far_rim[1].reshape(rows, KVH, HD)
    near_keys = near_rim[0].reshape(rows, KVH, HD)
    near_values = near_rim[1].reshape(rows, KVH, HD)
    far_scores = scores_of(query_heads, far_keys, far_allowed, score_scale)
    near_scores = scores_of(query_heads, near_keys, near_allowed, score_scale)
    row_max = jnp.maximum(
        own_max,
        jnp.maximum(
            jnp.max(far_scores, axis=-1, keepdims=True),
            jnp.max(near_scores, axis=-1, keepdims=True),
        ),
    )
    far_exp = jnp.exp(far_scores - row_max)
    near_exp = jnp.exp(near_scores - row_max)
    own_rescale = jnp.exp(own_max - row_max)
    row_sum = (
        own_sum * own_rescale
        + jnp.sum(far_exp, axis=-1, keepdims=True)
        + jnp.sum(near_exp, axis=-1, keepdims=True)
    )
    far_grad_p = jnp.einsum(
        "tghd,sgd->ghts", grad_heads, far_values, preferred_element_type=jnp.float32
    )
    near_grad_p = jnp.einsum(
        "tghd,sgd->ghts", grad_heads, near_values, preferred_element_type=jnp.float32
    )
    row_delta = (
        own_dot * own_rescale
        + jnp.sum(far_exp * far_grad_p, axis=-1, keepdims=True)
        + jnp.sum(near_exp * near_grad_p, axis=-1, keepdims=True)
    ) / row_sum
    far_grad_s = ((far_exp / row_sum) * (far_grad_p - row_delta)).astype(jnp.bfloat16)
    near_grad_s = ((near_exp / row_sum) * (near_grad_p - row_delta)).astype(jnp.bfloat16)
    far_key_grad = key_grad_of(far_grad_s, query_heads, score_scale).astype(jnp.bfloat16)
    far_back = shifted(far_key_grad, axes, -2)
    far_key_grad, near_grad_s = lax.optimization_barrier((far_key_grad, near_grad_s))
    near_key_grad = key_grad_of(near_grad_s, query_heads, score_scale).astype(jnp.bfloat16)
    near_back = shifted(near_key_grad, axes, -1)

    _, own_scale, row_delta, far_grad_s, near_grad_s = lax.optimization_barrier(
        ((far_key_grad, near_key_grad), own_rescale / row_sum, row_delta, far_grad_s, near_grad_s)
    )
    own_prob = own_exp * own_scale
    own_grad_s = (own_prob * (own_grad_p - row_delta)).astype(jnp.bfloat16)
    own_key_grad = key_grad_of(own_grad_s, query_heads, score_scale)
    query_grad = (
        query_grad_of(own_grad_s, own_keys)
        + query_grad_of(far_grad_s, far_keys)
        + query_grad_of(near_grad_s, near_keys)
    ) * score_scale
    query_grad = jnp.transpose(query_grad.astype(jnp.bfloat16), (2, 0, 1, 3)).reshape(rows, QH * HD)
    key_grad = own_key_grad + near_back.astype(jnp.float32) + far_back.astype(jnp.float32)
    key_grad = jnp.concatenate([key_grad[g] for g in range(KVH)], axis=1).astype(jnp.bfloat16)
    return (query_grad, key_grad)


def solution(mesh):
    placed = (
        P(("dp", "ctx", "uly"), None),
        P(("dp", "ctx", "uly"), None),
        P(("dp", "ctx", "uly"), None),
        P(("dp", "ctx", "uly"), None),
        P("dp"),
    )
    return jax.shard_map(
        body,
        mesh=mesh,
        in_specs=placed,
        out_specs=(P(("dp", "ctx", "uly"), None), P(("dp", "ctx", "uly"), None)),
        check_vma=False,
    )
```

```python
import jax
import jax.numpy as jnp
from jax import lax
from jax.sharding import PartitionSpec as P

QH = 32
KVH = 4
HD = 128
GROUP = 8
NEG = -1e30


def shifted(block, axis, distance):
    devices = range(lax.axis_size(axis))
    route = [(i - distance, i) for i in devices if i - distance in devices]
    return lax.ppermute(block, axis, route)


def doc_index(doc_lengths, positions):
    doc_ends = jnp.cumsum(doc_lengths)
    counted = jnp.sum((positions[:, None] >= doc_ends[None, :]).astype(jnp.int32), axis=1)
    return jnp.where(positions < 0, -1, counted)


def allowed_pairs(doc_lengths, query_pos, key_pos):
    query_docs = doc_index(doc_lengths, query_pos)
    key_docs = doc_index(doc_lengths, key_pos)
    return (query_docs[:, None] == key_docs[None, :]) & (key_pos[None, :] <= query_pos[:, None])


def scores_of(query_heads, key_heads, allowed, score_scale):
    scores = (
        jnp.einsum("tghd,sgd->ghts", query_heads, key_heads, preferred_element_type=jnp.float32)
        * score_scale
    )
    return jnp.where(allowed[None, None], scores, NEG)


def key_grad_of(grad_s, query_heads, score_scale):
    return (
        jnp.einsum("ghts,tghd->gsd", grad_s, query_heads, preferred_element_type=jnp.float32)
        * score_scale
    )


def query_grad_of(grad_s, keys):
    return jnp.einsum("ghts,sgd->ghtd", grad_s, keys, preferred_element_type=jnp.float32)


def body(queries, key_vectors, value_vectors, output_grad, doc_lengths):
    rows = queries.shape[0]
    score_scale = HD ** (-0.5)
    axes = ("ctx", "uly")
    key_value = jnp.stack([key_vectors, value_vectors])
    near_rim = shifted(key_value, axes, 1)
    far_rim = shifted(key_value, axes, 2)
    device_index = lax.axis_index(axes)
    query_heads = queries.reshape(rows, KVH, GROUP, HD)
    grad_heads = output_grad.reshape(rows, KVH, GROUP, HD)
    own_keys = key_vectors.reshape(rows, KVH, HD)
    own_values = value_vectors.reshape(rows, KVH, HD)
    query_pos = device_index * rows + jnp.arange(rows, dtype=jnp.int32)
    own_pos = query_pos
    own_allowed = allowed_pairs(doc_lengths, query_pos, own_pos)
    near_allowed = allowed_pairs(doc_lengths, query_pos, own_pos - rows)
    far_allowed = allowed_pairs(doc_lengths, query_pos, own_pos - 2 * rows)

    own_scores = scores_of(query_heads, own_keys, own_allowed, score_scale)
    own_max = jnp.max(own_scores, axis=-1, keepdims=True)
    own_exp = jnp.exp(own_scores - own_max)
    own_sum = jnp.sum(own_exp, axis=-1, keepdims=True)
    own_grad_p = jnp.einsum(
        "tghd,sgd->ghts", grad_heads, own_values, preferred_element_type=jnp.float32
    )
    own_dot = jnp.sum(own_exp * own_grad_p, axis=-1, keepdims=True)

    far_keys = far_rim[0].reshape(rows, KVH, HD)
    far_values = far_rim[1].reshape(rows, KVH, HD)
    near_keys = near_rim[0].reshape(rows, KVH, HD)
    near_values = near_rim[1].reshape(rows, KVH, HD)
    far_scores = scores_of(query_heads, far_keys, far_allowed, score_scale)
    near_scores = scores_of(query_heads, near_keys, near_allowed, score_scale)
    row_max = jnp.maximum(
        own_max,
        jnp.maximum(
            jnp.max(far_scores, axis=-1, keepdims=True),
            jnp.max(near_scores, axis=-1, keepdims=True),
        ),
    )
    far_exp = jnp.exp(far_scores - row_max)
    near_exp = jnp.exp(near_scores - row_max)
    own_rescale = jnp.exp(own_max - row_max)
    row_sum = (
        own_sum * own_rescale
        + jnp.sum(far_exp, axis=-1, keepdims=True)
        + jnp.sum(near_exp, axis=-1, keepdims=True)
    )
    far_grad_p = jnp.einsum(
        "tghd,sgd->ghts", grad_heads, far_values, preferred_element_type=jnp.float32
    )
    near_grad_p = jnp.einsum(
        "tghd,sgd->ghts", grad_heads, near_values, preferred_element_type=jnp.float32
    )
    row_delta = (
        own_dot * own_rescale
        + jnp.sum(far_exp * far_grad_p, axis=-1, keepdims=True)
        + jnp.sum(near_exp * near_grad_p, axis=-1, keepdims=True)
    ) / row_sum
    far_grad_s = ((far_exp / row_sum) * (far_grad_p - row_delta)).astype(jnp.bfloat16)
    near_grad_s = ((near_exp / row_sum) * (near_grad_p - row_delta)).astype(jnp.bfloat16)
    near_key_grad = key_grad_of(near_grad_s, query_heads, score_scale).astype(jnp.bfloat16)
    near_back = shifted(near_key_grad, axes, -1)
    near_key_grad, far_grad_s = lax.optimization_barrier((near_key_grad, far_grad_s))
    far_key_grad = key_grad_of(far_grad_s, query_heads, score_scale).astype(jnp.bfloat16)
    far_back = shifted(far_key_grad, axes, -2)

    _, own_scale, row_delta, far_grad_s, near_grad_s = lax.optimization_barrier(
        ((far_key_grad, near_key_grad), own_rescale / row_sum, row_delta, far_grad_s, near_grad_s)
    )
    own_prob = own_exp * own_scale
    own_grad_s = (own_prob * (own_grad_p - row_delta)).astype(jnp.bfloat16)
    own_key_grad = key_grad_of(own_grad_s, query_heads, score_scale)
    query_grad = (
        query_grad_of(own_grad_s, own_keys)
        + query_grad_of(far_grad_s, far_keys)
        + query_grad_of(near_grad_s, near_keys)
    ) * score_scale
    query_grad = jnp.transpose(query_grad.astype(jnp.bfloat16), (2, 0, 1, 3)).reshape(rows, QH * HD)
    key_grad = own_key_grad + near_back.astype(jnp.float32) + far_back.astype(jnp.float32)
    key_grad = jnp.concatenate([key_grad[g] for g in range(KVH)], axis=1).astype(jnp.bfloat16)
    return (query_grad, key_grad)


def solution(mesh):
    placed = (
        P(("dp", "ctx", "uly"), None),
        P(("dp", "ctx", "uly"), None),
        P(("dp", "ctx", "uly"), None),
        P(("dp", "ctx", "uly"), None),
        P("dp"),
    )
    return jax.shard_map(
        body,
        mesh=mesh,
        in_specs=placed,
        out_specs=(P(("dp", "ctx", "uly"), None), P(("dp", "ctx", "uly"), None)),
        check_vma=False,
    )
```

```python
import jax
import jax.numpy as jnp
from jax import lax
from jax.sharding import PartitionSpec as P

QH = 32
KVH = 4
HD = 128
GROUP = 8
NEG = -1e30


def shifted(block, axis, distance):
    devices = range(lax.axis_size(axis))
    route = [(i - distance, i) for i in devices if i - distance in devices]
    return lax.ppermute(block, axis, route)


def doc_index(doc_lengths, positions):
    doc_ends = jnp.cumsum(doc_lengths)
    counted = jnp.sum((positions[:, None] >= doc_ends[None, :]).astype(jnp.int32), axis=1)
    return jnp.where(positions < 0, -1, counted)


def allowed_pairs(doc_lengths, query_pos, key_pos):
    query_docs = doc_index(doc_lengths, query_pos)
    key_docs = doc_index(doc_lengths, key_pos)
    return (query_docs[:, None] == key_docs[None, :]) & (key_pos[None, :] <= query_pos[:, None])


def scores_of(query_heads, key_heads, allowed, score_scale):
    scores = (
        jnp.einsum("tghd,sgd->ghts", query_heads, key_heads, preferred_element_type=jnp.float32)
        * score_scale
    )
    return jnp.where(allowed[None, None], scores, NEG)


def key_grad_of(grad_s, query_heads, score_scale):
    return (
        jnp.einsum("ghts,tghd->gsd", grad_s, query_heads, preferred_element_type=jnp.float32)
        * score_scale
    )


def query_grad_of(grad_s, keys):
    return jnp.einsum("ghts,sgd->ghtd", grad_s, keys, preferred_element_type=jnp.float32)


def body(queries, key_vectors, value_vectors, output_grad, doc_lengths):
    rows = queries.shape[0]
    score_scale = HD ** (-0.5)
    axes = ("ctx", "uly")
    key_value = jnp.stack([key_vectors, value_vectors])
    near_rim = shifted(key_value, axes, 1)
    far_rim = shifted(key_value, axes, 2)
    device_index = lax.axis_index(axes)
    query_heads = queries.reshape(rows, KVH, GROUP, HD)
    grad_heads = output_grad.reshape(rows, KVH, GROUP, HD)
    own_keys = key_vectors.reshape(rows, KVH, HD)
    own_values = value_vectors.reshape(rows, KVH, HD)
    query_pos = device_index * rows + jnp.arange(rows, dtype=jnp.int32)
    own_pos = query_pos
    own_allowed = allowed_pairs(doc_lengths, query_pos, own_pos)
    near_allowed = allowed_pairs(doc_lengths, query_pos, own_pos - rows)
    far_allowed = allowed_pairs(doc_lengths, query_pos, own_pos - 2 * rows)

    own_scores = scores_of(query_heads, own_keys, own_allowed, score_scale)
    own_max = jnp.max(own_scores, axis=-1, keepdims=True)
    own_exp = jnp.exp(own_scores - own_max)
    own_sum = jnp.sum(own_exp, axis=-1, keepdims=True)
    own_grad_p = jnp.einsum(
        "tghd,sgd->ghts", grad_heads, own_values, preferred_element_type=jnp.float32
    )
    own_dot = jnp.sum(own_exp * own_grad_p, axis=-1, keepdims=True)

    near_keys = near_rim[0].reshape(rows, KVH, HD)
    near_values = near_rim[1].reshape(rows, KVH, HD)
    near_scores = scores_of(query_heads, near_keys, near_allowed, score_scale)
    near_max = jnp.max(near_scores, axis=-1, keepdims=True)
    near_exp = jnp.exp(near_scores - near_max)
    near_sum = jnp.sum(near_exp, axis=-1, keepdims=True)
    near_grad_p = jnp.einsum(
        "tghd,sgd->ghts", grad_heads, near_values, preferred_element_type=jnp.float32
    )
    near_dot = jnp.sum(near_exp * near_grad_p, axis=-1, keepdims=True)
    near_stats, far_rim = lax.optimization_barrier(
        ((near_max, near_exp, near_sum, near_grad_p, near_dot), far_rim)
    )
    near_max, near_exp, near_sum, near_grad_p, near_dot = near_stats

    far_keys = far_rim[0].reshape(rows, KVH, HD)
    far_values = far_rim[1].reshape(rows, KVH, HD)
    far_scores = scores_of(query_heads, far_keys, far_allowed, score_scale)
    row_max = jnp.maximum(
        jnp.maximum(own_max, near_max), jnp.max(far_scores, axis=-1, keepdims=True)
    )
    far_exp = jnp.exp(far_scores - row_max)
    own_rescale = jnp.exp(own_max - row_max)
    near_rescale = jnp.exp(near_max - row_max)
    row_sum = (
        own_sum * own_rescale
        + near_sum * near_rescale
        + jnp.sum(far_exp, axis=-1, keepdims=True)
    )
    far_grad_p = jnp.einsum(
        "tghd,sgd->ghts", grad_heads, far_values, preferred_element_type=jnp.float32
    )
    row_delta = (
        own_dot * own_rescale
        + near_dot * near_rescale
        + jnp.sum(far_exp * far_grad_p, axis=-1, keepdims=True)
    ) / row_sum
    near_exp = near_exp * near_rescale
    far_grad_s = ((far_exp / row_sum) * (far_grad_p - row_delta)).astype(jnp.bfloat16)
    near_grad_s = ((near_exp / row_sum) * (near_grad_p - row_delta)).astype(jnp.bfloat16)
    far_key_grad = key_grad_of(far_grad_s, query_heads, score_scale).astype(jnp.bfloat16)
    far_back = shifted(far_key_grad, axes, -2)
    far_key_grad, near_grad_s = lax.optimization_barrier((far_key_grad, near_grad_s))
    near_key_grad = key_grad_of(near_grad_s, query_heads, score_scale).astype(jnp.bfloat16)
    near_back = shifted(near_key_grad, axes, -1)

    _, own_scale, row_delta, far_grad_s, near_grad_s = lax.optimization_barrier(
        ((far_key_grad, near_key_grad), own_rescale / row_sum, row_delta, far_grad_s, near_grad_s)
    )
    own_prob = own_exp * own_scale
    own_grad_s = (own_prob * (own_grad_p - row_delta)).astype(jnp.bfloat16)
    own_key_grad = key_grad_of(own_grad_s, query_heads, score_scale)
    query_grad = (
        query_grad_of(own_grad_s, own_keys)
        + query_grad_of(far_grad_s, far_keys)
        + query_grad_of(near_grad_s, near_keys)
    ) * score_scale
    query_grad = jnp.transpose(query_grad.astype(jnp.bfloat16), (2, 0, 1, 3)).reshape(rows, QH * HD)
    key_grad = own_key_grad + near_back.astype(jnp.float32) + far_back.astype(jnp.float32)
    key_grad = jnp.concatenate([key_grad[g] for g in range(KVH)], axis=1).astype(jnp.bfloat16)
    return (query_grad, key_grad)


def solution(mesh):
    placed = (
        P(("dp", "ctx", "uly"), None),
        P(("dp", "ctx", "uly"), None),
        P(("dp", "ctx", "uly"), None),
        P(("dp", "ctx", "uly"), None),
        P("dp"),
    )
    return jax.shard_map(
        body,
        mesh=mesh,
        in_specs=placed,
        out_specs=(P(("dp", "ctx", "uly"), None), P(("dp", "ctx", "uly"), None)),
        check_vma=False,
    )
```

```python
import jax
import jax.numpy as jnp
from jax import lax
from jax.sharding import PartitionSpec as P

QH = 32
KVH = 4
HD = 128
GROUP = 8
NEG = -1e30


def shifted(block, axis, distance):
    devices = range(lax.axis_size(axis))
    route = [(i - distance, i) for i in devices if i - distance in devices]
    return lax.ppermute(block, axis, route)


def doc_index(doc_lengths, positions):
    doc_ends = jnp.cumsum(doc_lengths)
    counted = jnp.sum((positions[:, None] >= doc_ends[None, :]).astype(jnp.int32), axis=1)
    return jnp.where(positions < 0, -1, counted)


def allowed_pairs(doc_lengths, query_pos, key_pos):
    query_docs = doc_index(doc_lengths, query_pos)
    key_docs = doc_index(doc_lengths, key_pos)
    return (query_docs[:, None] == key_docs[None, :]) & (key_pos[None, :] <= query_pos[:, None])


def scores_of(query_heads, key_heads, allowed, score_scale):
    scores = (
        jnp.einsum("tghd,sgd->ghts", query_heads, key_heads, preferred_element_type=jnp.float32)
        * score_scale
    )
    return jnp.where(allowed[None, None], scores, NEG)


def key_grad_of(grad_s, query_heads, score_scale):
    return (
        jnp.einsum("ghts,tghd->gsd", grad_s, query_heads, preferred_element_type=jnp.float32)
        * score_scale
    )


def query_grad_of(grad_s, keys):
    return jnp.einsum("ghts,sgd->ghtd", grad_s, keys, preferred_element_type=jnp.float32)


def body(queries, key_vectors, value_vectors, output_grad, doc_lengths):
    rows = queries.shape[0]
    score_scale = HD ** (-0.5)
    axes = ("ctx", "uly")
    key_value = jnp.stack([key_vectors, value_vectors])
    near_rim = shifted(key_value, axes, 1)
    far_rim = shifted(lax.optimization_barrier(key_value), axes, 2)
    device_index = lax.axis_index(axes)
    query_heads = queries.reshape(rows, KVH, GROUP, HD)
    grad_heads = output_grad.reshape(rows, KVH, GROUP, HD)
    own_keys = key_vectors.reshape(rows, KVH, HD)
    own_values = value_vectors.reshape(rows, KVH, HD)
    query_pos = device_index * rows + jnp.arange(rows, dtype=jnp.int32)
    own_pos = query_pos
    own_allowed = allowed_pairs(doc_lengths, query_pos, own_pos)
    near_allowed = allowed_pairs(doc_lengths, query_pos, own_pos - rows)
    far_allowed = allowed_pairs(doc_lengths, query_pos, own_pos - 2 * rows)

    own_scores = scores_of(query_heads, own_keys, own_allowed, score_scale)
    own_max = jnp.max(own_scores, axis=-1, keepdims=True)
    own_exp = jnp.exp(own_scores - own_max)
    own_sum = jnp.sum(own_exp, axis=-1, keepdims=True)
    own_grad_p = jnp.einsum(
        "tghd,sgd->ghts", grad_heads, own_values, preferred_element_type=jnp.float32
    )
    own_dot = jnp.sum(own_exp * own_grad_p, axis=-1, keepdims=True)

    near_keys = near_rim[0].reshape(rows, KVH, HD)
    near_values = near_rim[1].reshape(rows, KVH, HD)
    near_scores = scores_of(query_heads, near_keys, near_allowed, score_scale)
    near_max = jnp.max(near_scores, axis=-1, keepdims=True)
    near_exp = jnp.exp(near_scores - near_max)
    near_sum = jnp.sum(near_exp, axis=-1, keepdims=True)
    near_grad_p = jnp.einsum(
        "tghd,sgd->ghts", grad_heads, near_values, preferred_element_type=jnp.float32
    )
    near_dot = jnp.sum(near_exp * near_grad_p, axis=-1, keepdims=True)
    near_stats, far_rim = lax.optimization_barrier(
        ((near_max, near_exp, near_sum, near_grad_p, near_dot), far_rim)
    )
    near_max, near_exp, near_sum, near_grad_p, near_dot = near_stats

    far_keys = far_rim[0].reshape(rows, KVH, HD)
    far_values = far_rim[1].reshape(rows, KVH, HD)
    far_scores = scores_of(query_heads, far_keys, far_allowed, score_scale)
    row_max = jnp.maximum(
        jnp.maximum(own_max, near_max), jnp.max(far_scores, axis=-1, keepdims=True)
    )
    far_exp = jnp.exp(far_scores - row_max)
    own_rescale = jnp.exp(own_max - row_max)
    near_rescale = jnp.exp(near_max - row_max)
    row_sum = (
        own_sum * own_rescale
        + near_sum * near_rescale
        + jnp.sum(far_exp, axis=-1, keepdims=True)
    )
    far_grad_p = jnp.einsum(
        "tghd,sgd->ghts", grad_heads, far_values, preferred_element_type=jnp.float32
    )
    row_delta = (
        own_dot * own_rescale
        + near_dot * near_rescale
        + jnp.sum(far_exp * far_grad_p, axis=-1, keepdims=True)
    ) / row_sum
    near_exp = near_exp * near_rescale
    far_grad_s = ((far_exp / row_sum) * (far_grad_p - row_delta)).astype(jnp.bfloat16)
    near_grad_s = ((near_exp / row_sum) * (near_grad_p - row_delta)).astype(jnp.bfloat16)
    far_key_grad = key_grad_of(far_grad_s, query_heads, score_scale).astype(jnp.bfloat16)
    far_back = shifted(far_key_grad, axes, -2)
    far_key_grad, near_grad_s = lax.optimization_barrier((far_key_grad, near_grad_s))
    near_key_grad = key_grad_of(near_grad_s, query_heads, score_scale).astype(jnp.bfloat16)
    near_back = shifted(near_key_grad, axes, -1)

    _, own_scale, row_delta, far_grad_s, near_grad_s = lax.optimization_barrier(
        ((far_key_grad, near_key_grad), own_rescale / row_sum, row_delta, far_grad_s, near_grad_s)
    )
    own_prob = own_exp * own_scale
    own_grad_s = (own_prob * (own_grad_p - row_delta)).astype(jnp.bfloat16)
    own_key_grad = key_grad_of(own_grad_s, query_heads, score_scale)
    query_grad = (
        query_grad_of(own_grad_s, own_keys)
        + query_grad_of(far_grad_s, far_keys)
        + query_grad_of(near_grad_s, near_keys)
    ) * score_scale
    query_grad = jnp.transpose(query_grad.astype(jnp.bfloat16), (2, 0, 1, 3)).reshape(rows, QH * HD)
    key_grad = own_key_grad + near_back.astype(jnp.float32) + far_back.astype(jnp.float32)
    key_grad = jnp.concatenate([key_grad[g] for g in range(KVH)], axis=1).astype(jnp.bfloat16)
    return (query_grad, key_grad)


def solution(mesh):
    placed = (
        P(("dp", "ctx", "uly"), None),
        P(("dp", "ctx", "uly"), None),
        P(("dp", "ctx", "uly"), None),
        P(("dp", "ctx", "uly"), None),
        P("dp"),
    )
    return jax.shard_map(
        body,
        mesh=mesh,
        in_specs=placed,
        out_specs=(P(("dp", "ctx", "uly"), None), P(("dp", "ctx", "uly"), None)),
        check_vma=False,
    )
```

```python
import jax
import jax.numpy as jnp
from jax import lax
from jax.sharding import PartitionSpec as P

QH = 32
KVH = 4
HD = 128
GROUP = 8
NEG = -1e30


def shifted(block, axis, distance):
    devices = range(lax.axis_size(axis))
    route = [(i - distance, i) for i in devices if i - distance in devices]
    return lax.ppermute(block, axis, route)


def doc_index(doc_lengths, positions):
    doc_ends = jnp.cumsum(doc_lengths)
    counted = jnp.sum((positions[:, None] >= doc_ends[None, :]).astype(jnp.int32), axis=1)
    return jnp.where(positions < 0, -1, counted)


def allowed_pairs(doc_lengths, query_pos, key_pos):
    query_docs = doc_index(doc_lengths, query_pos)
    key_docs = doc_index(doc_lengths, key_pos)
    return (query_docs[:, None] == key_docs[None, :]) & (key_pos[None, :] <= query_pos[:, None])


def scores_of(query_heads, key_heads, allowed, score_scale):
    scores = (
        jnp.einsum("tghd,sgd->ghts", query_heads, key_heads, preferred_element_type=jnp.float32)
        * score_scale
    )
    return jnp.where(allowed[None, None], scores, NEG)


def key_grad_of(grad_s, query_heads, score_scale):
    return (
        jnp.einsum("ghts,tghd->gsd", grad_s, query_heads, preferred_element_type=jnp.float32)
        * score_scale
    )


def query_grad_of(grad_s, keys):
    return jnp.einsum("ghts,sgd->ghtd", grad_s, keys, preferred_element_type=jnp.float32)


def body(queries, key_vectors, value_vectors, output_grad, doc_lengths):
    rows = queries.shape[0]
    score_scale = HD ** (-0.5)
    axes = ("ctx", "uly")
    key_value = jnp.stack([key_vectors, value_vectors])
    near_rim = shifted(key_value, axes, 1)
    far_sources = lax.optimization_barrier((key_vectors, value_vectors, key_value))[:2]
    far_rim = tuple(shifted(source, axes, 2) for source in far_sources)
    device_index = lax.axis_index(axes)
    query_heads = queries.reshape(rows, KVH, GROUP, HD)
    grad_heads = output_grad.reshape(rows, KVH, GROUP, HD)
    own_keys = key_vectors.reshape(rows, KVH, HD)
    own_values = value_vectors.reshape(rows, KVH, HD)
    query_pos = device_index * rows + jnp.arange(rows, dtype=jnp.int32)
    own_pos = query_pos
    own_allowed = allowed_pairs(doc_lengths, query_pos, own_pos)
    near_allowed = allowed_pairs(doc_lengths, query_pos, own_pos - rows)
    far_allowed = allowed_pairs(doc_lengths, query_pos, own_pos - 2 * rows)

    own_scores = scores_of(query_heads, own_keys, own_allowed, score_scale)
    own_max = jnp.max(own_scores, axis=-1, keepdims=True)
    own_exp = jnp.exp(own_scores - own_max)
    own_sum = jnp.sum(own_exp, axis=-1, keepdims=True)
    own_grad_p = jnp.einsum(
        "tghd,sgd->ghts", grad_heads, own_values, preferred_element_type=jnp.float32
    )
    own_dot = jnp.sum(own_exp * own_grad_p, axis=-1, keepdims=True)

    near_keys = near_rim[0].reshape(rows, KVH, HD)
    near_values = near_rim[1].reshape(rows, KVH, HD)
    near_scores = scores_of(query_heads, near_keys, near_allowed, score_scale)
    near_max = jnp.max(near_scores, axis=-1, keepdims=True)
    near_exp = jnp.exp(near_scores - near_max)
    near_sum = jnp.sum(near_exp, axis=-1, keepdims=True)
    near_grad_p = jnp.einsum(
        "tghd,sgd->ghts", grad_heads, near_values, preferred_element_type=jnp.float32
    )
    near_dot = jnp.sum(near_exp * near_grad_p, axis=-1, keepdims=True)
    near_stats, far_rim = lax.optimization_barrier(
        ((near_max, near_exp, near_sum, near_grad_p, near_dot), far_rim)
    )
    near_max, near_exp, near_sum, near_grad_p, near_dot = near_stats

    far_keys = far_rim[0].reshape(rows, KVH, HD)
    far_values = far_rim[1].reshape(rows, KVH, HD)
    far_scores = scores_of(query_heads, far_keys, far_allowed, score_scale)
    row_max = jnp.maximum(
        jnp.maximum(own_max, near_max), jnp.max(far_scores, axis=-1, keepdims=True)
    )
    far_exp = jnp.exp(far_scores - row_max)
    own_rescale = jnp.exp(own_max - row_max)
    near_rescale = jnp.exp(near_max - row_max)
    row_sum = (
        own_sum * own_rescale
        + near_sum * near_rescale
        + jnp.sum(far_exp, axis=-1, keepdims=True)
    )
    far_grad_p = jnp.einsum(
        "tghd,sgd->ghts", grad_heads, far_values, preferred_element_type=jnp.float32
    )
    row_delta = (
        own_dot * own_rescale
        + near_dot * near_rescale
        + jnp.sum(far_exp * far_grad_p, axis=-1, keepdims=True)
    ) / row_sum
    near_exp = near_exp * near_rescale
    far_grad_s = ((far_exp / row_sum) * (far_grad_p - row_delta)).astype(jnp.bfloat16)
    near_grad_s = ((near_exp / row_sum) * (near_grad_p - row_delta)).astype(jnp.bfloat16)
    far_key_grad = key_grad_of(far_grad_s, query_heads, score_scale).astype(jnp.bfloat16)
    far_back = shifted(far_key_grad, axes, -2)
    far_key_grad, near_grad_s = lax.optimization_barrier((far_key_grad, near_grad_s))
    near_key_grad = key_grad_of(near_grad_s, query_heads, score_scale).astype(jnp.bfloat16)
    near_back = shifted(near_key_grad, axes, -1)

    _, own_scale, row_delta, far_grad_s, near_grad_s = lax.optimization_barrier(
        ((far_key_grad, near_key_grad), own_rescale / row_sum, row_delta, far_grad_s, near_grad_s)
    )
    own_prob = own_exp * own_scale
    own_grad_s = (own_prob * (own_grad_p - row_delta)).astype(jnp.bfloat16)
    own_key_grad = key_grad_of(own_grad_s, query_heads, score_scale)
    query_grad = (
        query_grad_of(own_grad_s, own_keys)
        + query_grad_of(far_grad_s, far_keys)
        + query_grad_of(near_grad_s, near_keys)
    ) * score_scale
    query_grad = jnp.transpose(query_grad.astype(jnp.bfloat16), (2, 0, 1, 3)).reshape(rows, QH * HD)
    key_grad = own_key_grad + near_back.astype(jnp.float32) + far_back.astype(jnp.float32)
    key_grad = jnp.concatenate([key_grad[g] for g in range(KVH)], axis=1).astype(jnp.bfloat16)
    return (query_grad, key_grad)


def solution(mesh):
    placed = (
        P(("dp", "ctx", "uly"), None),
        P(("dp", "ctx", "uly"), None),
        P(("dp", "ctx", "uly"), None),
        P(("dp", "ctx", "uly"), None),
        P("dp"),
    )
    return jax.shard_map(
        body,
        mesh=mesh,
        in_specs=placed,
        out_specs=(P(("dp", "ctx", "uly"), None), P(("dp", "ctx", "uly"), None)),
        check_vma=False,
    )
```

```python
import jax
import jax.numpy as jnp
from jax import lax
from jax.sharding import PartitionSpec as P

QH = 32
KVH = 4
HD = 128
GROUP = 8
NEG = -1e30


def shifted(block, axis, distance):
    devices = range(lax.axis_size(axis))
    route = [(i - distance, i) for i in devices if i - distance in devices]
    return lax.ppermute(block, axis, route)


def doc_index(doc_lengths, positions):
    doc_ends = jnp.cumsum(doc_lengths)
    counted = jnp.sum((positions[:, None] >= doc_ends[None, :]).astype(jnp.int32), axis=1)
    return jnp.where(positions < 0, -1, counted)


def allowed_pairs(doc_lengths, query_pos, key_pos):
    query_docs = doc_index(doc_lengths, query_pos)
    key_docs = doc_index(doc_lengths, key_pos)
    return (query_docs[:, None] == key_docs[None, :]) & (key_pos[None, :] <= query_pos[:, None])


def scores_of(query_heads, key_heads, allowed, score_scale):
    scores = (
        jnp.einsum("tghd,sgd->ghts", query_heads, key_heads, preferred_element_type=jnp.float32)
        * score_scale
    )
    return jnp.where(allowed[None, None], scores, NEG)


def key_grad_of(grad_s, query_heads, score_scale):
    return (
        jnp.einsum("ghts,tghd->gsd", grad_s, query_heads, preferred_element_type=jnp.float32)
        * score_scale
    )


def query_grad_of(grad_s, keys):
    return jnp.einsum("ghts,sgd->ghtd", grad_s, keys, preferred_element_type=jnp.float32)


def body(queries, key_vectors, value_vectors, output_grad, doc_lengths):
    rows = queries.shape[0]
    score_scale = HD ** (-0.5)
    axes = ("ctx", "uly")
    key_value = jnp.stack([key_vectors, value_vectors])
    near_rim = shifted(key_value, axes, 1)
    far_rim = shifted(lax.optimization_barrier(key_value), axes, 2)
    device_index = lax.axis_index(axes)
    query_heads = queries.reshape(rows, KVH, GROUP, HD)
    grad_heads = output_grad.reshape(rows, KVH, GROUP, HD)
    own_keys = key_vectors.reshape(rows, KVH, HD)
    own_values = value_vectors.reshape(rows, KVH, HD)
    query_pos = device_index * rows + jnp.arange(rows, dtype=jnp.int32)
    own_pos = query_pos
    own_allowed = allowed_pairs(doc_lengths, query_pos, own_pos)
    near_allowed = allowed_pairs(doc_lengths, query_pos, own_pos - rows)
    far_allowed = allowed_pairs(doc_lengths, query_pos, own_pos - 2 * rows)

    own_scores = scores_of(query_heads, own_keys, own_allowed, score_scale)
    own_max = jnp.max(own_scores, axis=-1, keepdims=True)
    own_exp = jnp.exp(own_scores - own_max)
    own_sum = jnp.sum(own_exp, axis=-1, keepdims=True)
    own_grad_p = jnp.einsum(
        "tghd,sgd->ghts", grad_heads, own_values, preferred_element_type=jnp.float32
    )
    own_dot = jnp.sum(own_exp * own_grad_p, axis=-1, keepdims=True)

    near_keys = near_rim[0].reshape(rows, KVH, HD)
    near_values = near_rim[1].reshape(rows, KVH, HD)
    near_scores = scores_of(query_heads, near_keys, near_allowed, score_scale)
    near_max = jnp.max(near_scores, axis=-1, keepdims=True)
    near_exp = jnp.exp(near_scores - near_max)
    near_sum = jnp.sum(near_exp, axis=-1, keepdims=True)
    near_grad_p = jnp.einsum(
        "tghd,sgd->ghts", grad_heads, near_values, preferred_element_type=jnp.float32
    )
    near_dot = jnp.sum(near_exp * near_grad_p, axis=-1, keepdims=True)
    near_stats, far_rim = lax.optimization_barrier(
        ((near_max, near_exp, near_sum, near_grad_p, near_dot), far_rim)
    )
    near_max, near_exp, near_sum, near_grad_p, near_dot = near_stats

    far_keys = far_rim[0].reshape(rows, KVH, HD)
    far_values = far_rim[1].reshape(rows, KVH, HD)
    far_scores = scores_of(query_heads, far_keys, far_allowed, score_scale)
    row_max = jnp.maximum(
        jnp.maximum(own_max, near_max), jnp.max(far_scores, axis=-1, keepdims=True)
    )
    far_exp = jnp.exp(far_scores - row_max)
    own_rescale = jnp.exp(own_max - row_max)
    near_rescale = jnp.exp(near_max - row_max)
    row_sum = (
        own_sum * own_rescale
        + near_sum * near_rescale
        + jnp.sum(far_exp, axis=-1, keepdims=True)
    )
    far_grad_p = jnp.einsum(
        "tghd,sgd->ghts", grad_heads, far_values, preferred_element_type=jnp.float32
    )
    row_delta = (
        own_dot * own_rescale
        + near_dot * near_rescale
        + jnp.sum(far_exp * far_grad_p, axis=-1, keepdims=True)
    ) / row_sum
    near_exp = near_exp * near_rescale
    far_grad_s = ((far_exp / row_sum) * (far_grad_p - row_delta)).astype(jnp.bfloat16)
    far_key_grad = key_grad_of(far_grad_s, query_heads, score_scale).astype(jnp.bfloat16)
    far_back = shifted(far_key_grad, axes, -2)
    far_key_grad, near_exp, near_grad_p, near_delta, near_sum = lax.optimization_barrier(
        (far_key_grad, near_exp, near_grad_p, row_delta, row_sum)
    )
    near_grad_s = ((near_exp / near_sum) * (near_grad_p - near_delta)).astype(jnp.bfloat16)
    near_key_grad = key_grad_of(near_grad_s, query_heads, score_scale).astype(jnp.bfloat16)
    near_back = shifted(near_key_grad, axes, -1)

    _, own_scale, row_delta, far_grad_s, near_grad_s = lax.optimization_barrier(
        ((far_key_grad, near_key_grad), own_rescale / row_sum, row_delta, far_grad_s, near_grad_s)
    )
    own_prob = own_exp * own_scale
    own_grad_s = (own_prob * (own_grad_p - row_delta)).astype(jnp.bfloat16)
    own_key_grad = key_grad_of(own_grad_s, query_heads, score_scale)
    query_grad = (
        query_grad_of(own_grad_s, own_keys)
        + query_grad_of(far_grad_s, far_keys)
        + query_grad_of(near_grad_s, near_keys)
    ) * score_scale
    query_grad = jnp.transpose(query_grad.astype(jnp.bfloat16), (2, 0, 1, 3)).reshape(rows, QH * HD)
    key_grad = own_key_grad + near_back.astype(jnp.float32) + far_back.astype(jnp.float32)
    key_grad = jnp.concatenate([key_grad[g] for g in range(KVH)], axis=1).astype(jnp.bfloat16)
    return (query_grad, key_grad)


def solution(mesh):
    placed = (
        P(("dp", "ctx", "uly"), None),
        P(("dp", "ctx", "uly"), None),
        P(("dp", "ctx", "uly"), None),
        P(("dp", "ctx", "uly"), None),
        P("dp"),
    )
    return jax.shard_map(
        body,
        mesh=mesh,
        in_specs=placed,
        out_specs=(P(("dp", "ctx", "uly"), None), P(("dp", "ctx", "uly"), None)),
        check_vma=False,
    )
```

```python
import jax
import jax.numpy as jnp
from jax import lax
from jax.sharding import PartitionSpec as P

QH = 32
KVH = 4
HD = 128
GROUP = 8
NEG = -1e30


def shifted(block, axis, distance):
    devices = range(lax.axis_size(axis))
    route = [(i - distance, i) for i in devices if i - distance in devices]
    return lax.ppermute(block, axis, route)


def doc_index(doc_lengths, positions):
    doc_ends = jnp.cumsum(doc_lengths)
    counted = jnp.sum((positions[:, None] >= doc_ends[None, :]).astype(jnp.int32), axis=1)
    return jnp.where(positions < 0, -1, counted)


def allowed_pairs(doc_lengths, query_pos, key_pos):
    query_docs = doc_index(doc_lengths, query_pos)
    key_docs = doc_index(doc_lengths, key_pos)
    return (query_docs[:, None] == key_docs[None, :]) & (key_pos[None, :] <= query_pos[:, None])


def scores_of(query_heads, key_heads, allowed, score_scale):
    scores = (
        jnp.einsum("tghd,sgd->ghts", query_heads, key_heads, preferred_element_type=jnp.float32)
        * score_scale
    )
    return jnp.where(allowed[None, None], scores, NEG)


def key_grad_of(grad_s, query_heads, score_scale):
    return (
        jnp.einsum("ghts,tghd->gsd", grad_s, query_heads, preferred_element_type=jnp.float32)
        * score_scale
    )


def query_grad_of(grad_s, keys):
    return jnp.einsum("ghts,sgd->ghtd", grad_s, keys, preferred_element_type=jnp.float32)


def body(queries, key_vectors, value_vectors, output_grad, doc_lengths):
    rows = queries.shape[0]
    score_scale = HD ** (-0.5)
    axes = ("ctx", "uly")
    key_value = jnp.stack([key_vectors, value_vectors])
    near_rim = shifted(key_value, axes, 1)
    far_rim = shifted(lax.optimization_barrier(key_value), axes, 2)
    device_index = lax.axis_index(axes)
    query_heads = queries.reshape(rows, KVH, GROUP, HD)
    grad_heads = output_grad.reshape(rows, KVH, GROUP, HD)
    own_keys = key_vectors.reshape(rows, KVH, HD)
    own_values = value_vectors.reshape(rows, KVH, HD)
    query_pos = device_index * rows + jnp.arange(rows, dtype=jnp.int32)
    own_pos = query_pos
    own_allowed = allowed_pairs(doc_lengths, query_pos, own_pos)
    near_allowed = allowed_pairs(doc_lengths, query_pos, own_pos - rows)
    far_allowed = allowed_pairs(doc_lengths, query_pos, own_pos - 2 * rows)

    own_scores = scores_of(query_heads, own_keys, own_allowed, score_scale)
    own_max = jnp.max(own_scores, axis=-1, keepdims=True)
    own_exp = jnp.exp(own_scores - own_max)
    own_sum = jnp.sum(own_exp, axis=-1, keepdims=True)
    own_grad_p = jnp.einsum(
        "tghd,sgd->ghts", grad_heads, own_values, preferred_element_type=jnp.float32
    )
    own_dot = jnp.sum(own_exp * own_grad_p, axis=-1, keepdims=True)

    near_keys = near_rim[0].reshape(rows, KVH, HD)
    near_values = near_rim[1].reshape(rows, KVH, HD)
    near_scores = scores_of(query_heads, near_keys, near_allowed, score_scale)
    near_max = jnp.max(near_scores, axis=-1, keepdims=True)
    near_exp = jnp.exp(near_scores - near_max)
    near_sum = jnp.sum(near_exp, axis=-1, keepdims=True)
    near_grad_p = jnp.einsum(
        "tghd,sgd->ghts", grad_heads, near_values, preferred_element_type=jnp.float32
    )
    near_dot = jnp.sum(near_exp * near_grad_p, axis=-1, keepdims=True)
    near_stats, far_rim = lax.optimization_barrier(
        ((near_max, near_exp, near_sum, near_grad_p, near_dot), far_rim)
    )
    near_max, near_exp, near_sum, near_grad_p, near_dot = near_stats

    far_keys = far_rim[0].reshape(rows, KVH, HD)
    far_values = far_rim[1].reshape(rows, KVH, HD)
    far_scores = scores_of(query_heads, far_keys, far_allowed, score_scale)
    row_max = jnp.maximum(
        jnp.maximum(own_max, near_max), jnp.max(far_scores, axis=-1, keepdims=True)
    )
    far_exp = jnp.exp(far_scores - row_max)
    own_rescale = jnp.exp(own_max - row_max)
    near_rescale = jnp.exp(near_max - row_max)
    row_sum = (
        own_sum * own_rescale
        + near_sum * near_rescale
        + jnp.sum(far_exp, axis=-1, keepdims=True)
    )
    far_grad_p = jnp.einsum(
        "tghd,sgd->ghts", grad_heads, far_values, preferred_element_type=jnp.float32
    )
    row_delta = (
        own_dot * own_rescale
        + near_dot * near_rescale
        + jnp.sum(far_exp * far_grad_p, axis=-1, keepdims=True)
    ) / row_sum
    near_exp = near_exp * near_rescale
    far_grad_s = ((far_exp / row_sum) * (far_grad_p - row_delta)).astype(jnp.bfloat16)
    near_grad_s = ((near_exp / row_sum) * (near_grad_p - row_delta)).astype(jnp.bfloat16)
    near_key_grad = key_grad_of(near_grad_s, query_heads, score_scale).astype(jnp.bfloat16)
    near_back = shifted(near_key_grad, axes, -1)
    near_key_grad, far_grad_s = lax.optimization_barrier((near_key_grad, far_grad_s))
    far_key_grad = key_grad_of(far_grad_s, query_heads, score_scale).astype(jnp.bfloat16)
    far_back = shifted(far_key_grad, axes, -2)

    _, own_scale, row_delta, far_grad_s, near_grad_s = lax.optimization_barrier(
        ((far_key_grad, near_key_grad), own_rescale / row_sum, row_delta, far_grad_s, near_grad_s)
    )
    own_prob = own_exp * own_scale
    own_grad_s = (own_prob * (own_grad_p - row_delta)).astype(jnp.bfloat16)
    own_key_grad = key_grad_of(own_grad_s, query_heads, score_scale)
    query_grad = (
        query_grad_of(own_grad_s, own_keys)
        + query_grad_of(far_grad_s, far_keys)
        + query_grad_of(near_grad_s, near_keys)
    ) * score_scale
    query_grad = jnp.transpose(query_grad.astype(jnp.bfloat16), (2, 0, 1, 3)).reshape(rows, QH * HD)
    key_grad = own_key_grad + near_back.astype(jnp.float32) + far_back.astype(jnp.float32)
    key_grad = jnp.concatenate([key_grad[g] for g in range(KVH)], axis=1).astype(jnp.bfloat16)
    return (query_grad, key_grad)


def solution(mesh):
    placed = (
        P(("dp", "ctx", "uly"), None),
        P(("dp", "ctx", "uly"), None),
        P(("dp", "ctx", "uly"), None),
        P(("dp", "ctx", "uly"), None),
        P("dp"),
    )
    return jax.shard_map(
        body,
        mesh=mesh,
        in_specs=placed,
        out_specs=(P(("dp", "ctx", "uly"), None), P(("dp", "ctx", "uly"), None)),
        check_vma=False,
    )
```

```python
import jax
import jax.numpy as jnp
from jax import lax
from jax.sharding import PartitionSpec as P

QH = 32
KVH = 4
HD = 128
GROUP = 8
NEG = -1e30


def shifted(block, axis, distance):
    devices = range(lax.axis_size(axis))
    route = [(i - distance, i) for i in devices if i - distance in devices]
    return lax.ppermute(block, axis, route)


def doc_index(doc_lengths, positions):
    doc_ends = jnp.cumsum(doc_lengths)
    counted = jnp.sum((positions[:, None] >= doc_ends[None, :]).astype(jnp.int32), axis=1)
    return jnp.where(positions < 0, -1, counted)


def allowed_pairs(doc_lengths, query_pos, key_pos):
    query_docs = doc_index(doc_lengths, query_pos)
    key_docs = doc_index(doc_lengths, key_pos)
    return (query_docs[:, None] == key_docs[None, :]) & (key_pos[None, :] <= query_pos[:, None])


def scores_of(query_heads, key_heads, allowed, score_scale):
    scores = (
        jnp.einsum("tghd,sgd->ghts", query_heads, key_heads, preferred_element_type=jnp.float32)
        * score_scale
    )
    return jnp.where(allowed[None, None], scores, NEG)


def key_grad_of(grad_s, query_heads, score_scale):
    return (
        jnp.einsum("ghts,tghd->gsd", grad_s, query_heads, preferred_element_type=jnp.float32)
        * score_scale
    )


def query_grad_of(grad_s, keys):
    return jnp.einsum("ghts,sgd->tghd", grad_s, keys, preferred_element_type=jnp.float32)


def body(queries, key_vectors, value_vectors, output_grad, doc_lengths):
    rows = queries.shape[0]
    score_scale = HD ** (-0.5)
    axes = ("ctx", "uly")
    key_value = jnp.stack([key_vectors, value_vectors])
    near_rim = shifted(key_value, axes, 1)
    far_rim = shifted(lax.optimization_barrier(key_value), axes, 2)
    device_index = lax.axis_index(axes)
    query_heads = queries.reshape(rows, KVH, GROUP, HD)
    grad_heads = output_grad.reshape(rows, KVH, GROUP, HD)
    own_keys = key_vectors.reshape(rows, KVH, HD)
    own_values = value_vectors.reshape(rows, KVH, HD)
    query_pos = device_index * rows + jnp.arange(rows, dtype=jnp.int32)
    own_pos = query_pos
    own_allowed = allowed_pairs(doc_lengths, query_pos, own_pos)
    near_allowed = allowed_pairs(doc_lengths, query_pos, own_pos - rows)
    far_allowed = allowed_pairs(doc_lengths, query_pos, own_pos - 2 * rows)

    own_scores = scores_of(query_heads, own_keys, own_allowed, score_scale)
    own_max = jnp.max(own_scores, axis=-1, keepdims=True)
    own_exp = jnp.exp(own_scores - own_max)
    own_sum = jnp.sum(own_exp, axis=-1, keepdims=True)
    own_grad_p = jnp.einsum(
        "tghd,sgd->ghts", grad_heads, own_values, preferred_element_type=jnp.float32
    )
    own_dot = jnp.sum(own_exp * own_grad_p, axis=-1, keepdims=True)

    near_keys = near_rim[0].reshape(rows, KVH, HD)
    near_values = near_rim[1].reshape(rows, KVH, HD)
    near_scores = scores_of(query_heads, near_keys, near_allowed, score_scale)
    near_max = jnp.max(near_scores, axis=-1, keepdims=True)
    near_exp = jnp.exp(near_scores - near_max)
    near_sum = jnp.sum(near_exp, axis=-1, keepdims=True)
    near_grad_p = jnp.einsum(
        "tghd,sgd->ghts", grad_heads, near_values, preferred_element_type=jnp.float32
    )
    near_dot = jnp.sum(near_exp * near_grad_p, axis=-1, keepdims=True)
    near_stats, far_rim = lax.optimization_barrier(
        ((near_max, near_exp, near_sum, near_grad_p, near_dot), far_rim)
    )
    near_max, near_exp, near_sum, near_grad_p, near_dot = near_stats

    far_keys = far_rim[0].reshape(rows, KVH, HD)
    far_values = far_rim[1].reshape(rows, KVH, HD)
    far_scores = scores_of(query_heads, far_keys, far_allowed, score_scale)
    row_max = jnp.maximum(
        jnp.maximum(own_max, near_max), jnp.max(far_scores, axis=-1, keepdims=True)
    )
    far_exp = jnp.exp(far_scores - row_max)
    own_rescale = jnp.exp(own_max - row_max)
    near_rescale = jnp.exp(near_max - row_max)
    row_sum = (
        own_sum * own_rescale
        + near_sum * near_rescale
        + jnp.sum(far_exp, axis=-1, keepdims=True)
    )
    far_grad_p = jnp.einsum(
        "tghd,sgd->ghts", grad_heads, far_values, preferred_element_type=jnp.float32
    )
    row_delta = (
        own_dot * own_rescale
        + near_dot * near_rescale
        + jnp.sum(far_exp * far_grad_p, axis=-1, keepdims=True)
    ) / row_sum
    near_exp = near_exp * near_rescale
    far_grad_s = ((far_exp / row_sum) * (far_grad_p - row_delta)).astype(jnp.bfloat16)
    near_grad_s = ((near_exp / row_sum) * (near_grad_p - row_delta)).astype(jnp.bfloat16)
    far_key_grad = key_grad_of(far_grad_s, query_heads, score_scale).astype(jnp.bfloat16)
    far_back = shifted(far_key_grad, axes, -2)
    far_key_grad, near_grad_s = lax.optimization_barrier((far_key_grad, near_grad_s))
    near_key_grad = key_grad_of(near_grad_s, query_heads, score_scale).astype(jnp.bfloat16)
    near_back = shifted(near_key_grad, axes, -1)

    _, own_scale, row_delta, far_grad_s, near_grad_s = lax.optimization_barrier(
        ((far_key_grad, near_key_grad), own_rescale / row_sum, row_delta, far_grad_s, near_grad_s)
    )
    own_prob = own_exp * own_scale
    own_grad_s = (own_prob * (own_grad_p - row_delta)).astype(jnp.bfloat16)
    own_key_grad = key_grad_of(own_grad_s, query_heads, score_scale)
    query_grad = (
        query_grad_of(own_grad_s, own_keys)
        + query_grad_of(far_grad_s, far_keys)
        + query_grad_of(near_grad_s, near_keys)
    ) * score_scale
    query_grad = query_grad.astype(jnp.bfloat16).reshape(rows, QH * HD)
    key_grad = own_key_grad + near_back.astype(jnp.float32) + far_back.astype(jnp.float32)
    key_grad = jnp.concatenate([key_grad[g] for g in range(KVH)], axis=1).astype(jnp.bfloat16)
    return (query_grad, key_grad)


def solution(mesh):
    placed = (
        P(("dp", "ctx", "uly"), None),
        P(("dp", "ctx", "uly"), None),
        P(("dp", "ctx", "uly"), None),
        P(("dp", "ctx", "uly"), None),
        P("dp"),
    )
    return jax.shard_map(
        body,
        mesh=mesh,
        in_specs=placed,
        out_specs=(P(("dp", "ctx", "uly"), None), P(("dp", "ctx", "uly"), None)),
        check_vma=False,
    )
```

```python
import jax
import jax.numpy as jnp
from jax import lax
from jax.sharding import PartitionSpec as P

QH = 32
KVH = 4
HD = 128
GROUP = 8
NEG = -1e30


def shifted(block, axis, distance):
    devices = range(lax.axis_size(axis))
    route = [(i - distance, i) for i in devices if i - distance in devices]
    return lax.ppermute(block, axis, route)


def doc_index(doc_lengths, positions):
    doc_ends = jnp.cumsum(doc_lengths)
    counted = jnp.sum((positions[:, None] >= doc_ends[None, :]).astype(jnp.int32), axis=1)
    return jnp.where(positions < 0, -1, counted)


def allowed_pairs(doc_lengths, query_pos, key_pos):
    query_docs = doc_index(doc_lengths, query_pos)
    key_docs = doc_index(doc_lengths, key_pos)
    return (query_docs[:, None] == key_docs[None, :]) & (key_pos[None, :] <= query_pos[:, None])


def scores_of(query_heads, key_heads, allowed, score_scale):
    scores = (
        jnp.einsum("tghd,sgd->ghts", query_heads, key_heads, preferred_element_type=jnp.float32)
        * score_scale
    )
    return jnp.where(allowed[None, None], scores, NEG)


def key_grad_of(grad_s, query_heads, score_scale):
    return (
        jnp.einsum("ghts,tghd->gsd", grad_s, query_heads, preferred_element_type=jnp.float32)
        * score_scale
    )


def query_grad_of(grad_s, keys):
    return jnp.einsum("ghts,sgd->tghd", grad_s, keys, preferred_element_type=jnp.float32)


def body(queries, key_vectors, value_vectors, output_grad, doc_lengths):
    rows = queries.shape[0]
    score_scale = HD ** (-0.5)
    axes = ("ctx", "uly")
    key_value = jnp.stack([key_vectors, value_vectors])
    near_rim = shifted(key_value, axes, 1)
    far_rim = shifted(lax.optimization_barrier(key_value), axes, 2)
    device_index = lax.axis_index(axes)
    query_heads = queries.reshape(rows, KVH, GROUP, HD)
    grad_heads = output_grad.reshape(rows, KVH, GROUP, HD)
    own_keys = key_vectors.reshape(rows, KVH, HD)
    own_values = value_vectors.reshape(rows, KVH, HD)
    query_pos = device_index * rows + jnp.arange(rows, dtype=jnp.int32)
    own_pos = query_pos
    own_allowed = allowed_pairs(doc_lengths, query_pos, own_pos)
    near_allowed = allowed_pairs(doc_lengths, query_pos, own_pos - rows)
    far_allowed = allowed_pairs(doc_lengths, query_pos, own_pos - 2 * rows)

    own_scores = scores_of(query_heads, own_keys, own_allowed, score_scale)
    own_max = jnp.max(own_scores, axis=-1, keepdims=True)
    own_exp = jnp.exp(own_scores - own_max)
    own_sum = jnp.sum(own_exp, axis=-1, keepdims=True)
    own_grad_p = jnp.einsum(
        "tghd,sgd->ghts", grad_heads, own_values, preferred_element_type=jnp.float32
    )
    own_dot = jnp.sum(own_exp * own_grad_p, axis=-1, keepdims=True)

    near_keys = near_rim[0].reshape(rows, KVH, HD)
    near_values = near_rim[1].reshape(rows, KVH, HD)
    near_scores = scores_of(query_heads, near_keys, near_allowed, score_scale)
    near_max = jnp.max(near_scores, axis=-1, keepdims=True)
    near_exp = jnp.exp(near_scores - near_max)
    near_sum = jnp.sum(near_exp, axis=-1, keepdims=True)
    near_grad_p = jnp.einsum(
        "tghd,sgd->ghts", grad_heads, near_values, preferred_element_type=jnp.float32
    )
    near_dot = jnp.sum(near_exp * near_grad_p, axis=-1, keepdims=True)
    near_stats, far_rim = lax.optimization_barrier(
        ((near_max, near_exp, near_sum, near_grad_p, near_dot), far_rim)
    )
    near_max, near_exp, near_sum, near_grad_p, near_dot = near_stats

    far_keys = far_rim[0].reshape(rows, KVH, HD)
    far_values = far_rim[1].reshape(rows, KVH, HD)
    far_scores = scores_of(query_heads, far_keys, far_allowed, score_scale)
    row_max = jnp.maximum(
        jnp.maximum(own_max, near_max), jnp.max(far_scores, axis=-1, keepdims=True)
    )
    far_exp = jnp.exp(far_scores - row_max)
    own_rescale = jnp.exp(own_max - row_max)
    near_rescale = jnp.exp(near_max - row_max)
    row_sum = (
        own_sum * own_rescale
        + near_sum * near_rescale
        + jnp.sum(far_exp, axis=-1, keepdims=True)
    )
    far_grad_p = jnp.einsum(
        "tghd,sgd->ghts", grad_heads, far_values, preferred_element_type=jnp.float32
    )
    row_delta = (
        own_dot * own_rescale
        + near_dot * near_rescale
        + jnp.sum(far_exp * far_grad_p, axis=-1, keepdims=True)
    ) / row_sum
    far_grad_s = ((far_exp / row_sum) * (far_grad_p - row_delta)).astype(jnp.bfloat16)
    near_grad_s = ((near_exp * (near_rescale / row_sum)) * (near_grad_p - row_delta)).astype(
        jnp.bfloat16
    )
    far_key_grad = key_grad_of(far_grad_s, query_heads, score_scale).astype(jnp.bfloat16)
    far_back = shifted(far_key_grad, axes, -2)
    far_key_grad, near_grad_s = lax.optimization_barrier((far_key_grad, near_grad_s))
    near_key_grad = key_grad_of(near_grad_s, query_heads, score_scale).astype(jnp.bfloat16)
    near_back = shifted(near_key_grad, axes, -1)

    _, own_scale, row_delta, far_grad_s, near_grad_s = lax.optimization_barrier(
        ((far_key_grad, near_key_grad), own_rescale / row_sum, row_delta, far_grad_s, near_grad_s)
    )
    own_prob = own_exp * own_scale
    own_grad_s = (own_prob * (own_grad_p - row_delta)).astype(jnp.bfloat16)
    own_key_grad = key_grad_of(own_grad_s, query_heads, score_scale)
    query_grad = (
        query_grad_of(own_grad_s, own_keys)
        + query_grad_of(far_grad_s, far_keys)
        + query_grad_of(near_grad_s, near_keys)
    ) * score_scale
    query_grad = query_grad.astype(jnp.bfloat16).reshape(rows, QH * HD)
    key_grad = own_key_grad + near_back.astype(jnp.float32) + far_back.astype(jnp.float32)
    key_grad = jnp.concatenate([key_grad[g] for g in range(KVH)], axis=1).astype(jnp.bfloat16)
    return (query_grad, key_grad)


def solution(mesh):
    placed = (
        P(("dp", "ctx", "uly"), None),
        P(("dp", "ctx", "uly"), None),
        P(("dp", "ctx", "uly"), None),
        P(("dp", "ctx", "uly"), None),
        P("dp"),
    )
    return jax.shard_map(
        body,
        mesh=mesh,
        in_specs=placed,
        out_specs=(P(("dp", "ctx", "uly"), None), P(("dp", "ctx", "uly"), None)),
        check_vma=False,
    )
```
